512 devices in a mesh: member: 16 (over x_lo, y), dp: 32 (over z, x_hi, core).
Axes of the slice: x: 4 (x_hi: 2, x_lo: 2; x = x_hi * 2 + x_lo), y: 8, z: 8, core: 2. Of those that a mesh axis runs over, the one named last changes fastest.
Arguments:
- inputs: bfloat16 [8192, 64], P('dp'), may hold values from -6 to 6
- observed: float32 [64, 8192], P('member', 'dp'), may hold values from -6 to 6
- noise: bfloat16 [2, 32, 64, 8192], P(None, None, 'member', 'dp'), may hold values from -4 to 4
- w_in: float32 [32, 64, 4096], P('member', None, 'dp'), may hold values from -0.75 to 0.75
- b_in: float32 [32, 4096], P('member', 'dp'), may hold values from -3 to 3
- w_out: float32 [32, 64, 4096], P('member', None, 'dp'), may hold values from -0.09375 to 0.09375
- b_out: float32 [32, 64], P('member'), may hold values from -3 to 3
Outputs:
- new_w_in: float32 [32, 64, 4096], P('member', None, 'dp')
- new_b_in: float32 [32, 4096], P('member', 'dp')
- new_w_out: float32 [32, 64, 4096], P('member', None, 'dp')
- new_b_out: float32 [32, 64], P('member')
The draws below stay inside these ranges and needn't reach their ends.
All inputs are finite; a program needn't handle non-finite values.
Results may differ from the reference program's by a relative error of at most 0.00056.
Values may be sent and summed in bfloat16 or wider, within the bound.
No kernel may reach another device: no remote copies, remote signals or barrier semaphores. Data moves between devices by JAX's collectives and lax.ppermute only.
A program may use at most 64 MiB of HBM per device.

```python
import jax
import jax.numpy as jnp
from jax import lax

F_IN = 64
H = 4096
O = 64
UPDATES = 2
MEMBERS = 32
SAMPLES = 8192


def with_spikes(values, key, source, target, shards_of, factor):
    def block_of(dim):
        return (jnp.arange(values.shape[dim]) // (values.shape[dim] // shards_of)).reshape((-1,) + (1,) * (values.ndim - 1 - dim))

    near = jax.random.permutation(key, shards_of)[block_of(target)]
    second = (block_of(target) + shards_of // 2) % shards_of
    return jnp.where((block_of(source) == near) | (block_of(source) == second), factor * values, values)


def levels(rng, shape, pieces, smallest, largest):
    def one(position, parts):
        heights = jax.random.uniform(jax.random.fold_in(jax.random.fold_in(rng, 6), position), (parts,), jnp.float32, smallest / len(pieces), largest / len(pieces))
        return jnp.repeat(jnp.exp(heights), shape[position] // parts).reshape((-1,) + (1,) * (len(shape) - position - 1))

    loudness = one(*pieces[0])
    for cut in pieces[1:]:
        loudness = loudness * one(*cut)
    return loudness


def scatter_about(rng, extent, width, limit, cuts=(), held_as=jnp.bfloat16):
    result = width * jax.random.normal(rng, extent, jnp.float32)
    if cuts:
        result = result * levels(rng, extent, cuts, -0.22, 0.18)
    return jnp.clip(result, -limit, limit).astype(held_as)


def heavy_noise(key, extent, deviation, limit, shards, heavy, kind=jnp.bfloat16):
    entries = deviation * jax.random.normal(key, extent, jnp.float32)
    if shards:
        entries = entries * levels(key, extent, shards, -0.22, 0.18)
    return jnp.clip(with_spikes(entries, jax.random.fold_in(key, 3), *heavy), -limit, limit).astype(kind)


def setup_inputs(seed: int = 0) -> dict:
    arg_keys = jax.random.split(jax.random.key(seed), 8)
    inputs = scatter_about(arg_keys[0], (SAMPLES, F_IN), 1.0, 6.0, ((0, 32),))
    observed = scatter_about(arg_keys[1], (O, SAMPLES), 1.0, 6.0, ((0, 16), (1, 32)), jnp.float32)
    noise = heavy_noise(arg_keys[2], (UPDATES, MEMBERS, O, SAMPLES), 0.5, 4.0, ((2, 16), (3, 32)), (3, 1, 32, 2.75))
    w_in = scatter_about(arg_keys[3], (MEMBERS, F_IN, H), F_IN ** -0.5, 0.75, ((0, 16), (2, 32)), jnp.float32)
    b_in = scatter_about(arg_keys[4], (MEMBERS, H), 0.5, 3.0, ((0, 16), (1, 32)), jnp.float32)
    w_out = scatter_about(arg_keys[5], (MEMBERS, O, H), H ** -0.5, 0.09375, ((0, 16), (2, 32)), jnp.float32)
    b_out = scatter_about(arg_keys[6], (MEMBERS, O), 0.5, 3.0, ((0, 16),), jnp.float32)
    return {"inputs": inputs, "observed": observed, "noise": noise, "w_in": w_in, "b_in": b_in, "w_out": w_out, "b_out": b_out}


ridge_level = 0.5

def forward(inputs, w_in, b_in, w_out, b_out):

    def single(item):
        weight_in, bias_in, weight_out, bias_out = item
        rounded_bias = lax.optimization_barrier(bias_in.astype(jnp.bfloat16))
        pre = jnp.dot(inputs.astype(jnp.float32), weight_in.astype(jnp.bfloat16).astype(jnp.float32), preferred_element_type=jnp.float32) + rounded_bias.astype(jnp.float32)[None, :]
        hidden = jnp.tanh(pre).astype(jnp.bfloat16)
        predicted = lax.dot_general(weight_out.astype(jnp.bfloat16).astype(jnp.float32), hidden.astype(jnp.float32), (((1,), (1,)), ((), ())), preferred_element_type=jnp.float32)
        return predicted + bias_out[:, None]
    return lax.map(single, (w_in, b_in, w_out, b_out))

def solve_gain(gram, cross):
    eye = jnp.eye(gram.shape[0], dtype=gram.dtype)
    factor = jnp.linalg.cholesky(gram + ridge_level * eye)
    middle = lax.linalg.triangular_solve(factor, cross, left_side=True, lower=True)
    return lax.linalg.triangular_solve(factor, middle, left_side=True, lower=True, transpose_a=True)

def blend(param, gain):
    flat = param.reshape(param.shape[0], -1)
    moved = lax.dot_general(gain, flat, (((0,), (0,)), ((), ())), precision=lax.Precision.HIGHEST)
    return param + moved.reshape(param.shape)

def reference(inputs, observed, noise, w_in, b_in, w_out, b_out):
    count = observed.shape[0] * observed.shape[1]
    for update in range(UPDATES):
        predicted = forward(inputs, w_in, b_in, w_out, b_out)
        mean_pred = jnp.mean(predicted, axis=0)
        anomaly = (predicted - mean_pred[None]).reshape(predicted.shape[0], -1)
        misfit = (observed[None] + noise[update].astype(jnp.float32) - predicted).reshape(predicted.shape[0], -1)
        gram = lax.dot_general(anomaly, anomaly, (((1,), (1,)), ((), ())), precision=lax.Precision.HIGHEST) / count
        cross = lax.dot_general(anomaly, misfit, (((1,), (1,)), ((), ())), precision=lax.Precision.HIGHEST) / count
        gain = solve_gain(gram, cross)
        w_in = blend(w_in, gain)
        b_in = blend(b_in, gain)
        w_out = blend(w_out, gain)
        b_out = blend(b_out, gain)
    return (w_in, b_in, w_out, b_out)
```

```python
import jax
import jax.numpy as jnp
from jax import lax
from jax.sharding import PartitionSpec as P

UPDATES = 2


ridge_level = 0.5


def solve_gain(gram, cross):
    eye = jnp.eye(gram.shape[0], dtype=gram.dtype)
    factor = jnp.linalg.cholesky(gram + ridge_level * eye)
    middle = lax.linalg.triangular_solve(factor, cross, left_side=True, lower=True)
    return lax.linalg.triangular_solve(factor, middle, left_side=True, lower=True, transpose_a=True)


def pack(w_in, b_in, w_out, b_out):
    n = w_in.shape[0]
    return jnp.concatenate(
        [w_in.reshape(n, -1), w_out.reshape(n, -1), b_in.reshape(n, -1), b_out.reshape(n, -1)], axis=1
    )


def unpack(flat, f_in, hid, outs):
    n = flat.shape[0]
    a = f_in * hid
    b = a + outs * hid
    c = b + hid
    return (
        flat[:, :a].reshape(n, f_in, hid),
        flat[:, b:c].reshape(n, hid),
        flat[:, a:b].reshape(n, outs, hid),
        flat[:, c:].reshape(n, outs),
    )


def predict(inputs, own_flat, b_out, f_in, hid, outs):
    n = own_flat.shape[0]
    a = f_in * hid
    b = a + outs * hid
    rounded = own_flat[:, : b + hid].astype(jnp.bfloat16)
    gathered = lax.all_gather(rounded, "dp", axis=0, tiled=False)
    d = gathered.shape[0]
    w_in = gathered[:, :, :a].reshape(d, n, f_in, hid)
    w_out = gathered[:, :, a:b].reshape(d, n, outs, hid)
    b_in = gathered[:, :, b : b + hid]
    pre = jnp.einsum("sf,dnfh->nsdh", inputs, w_in, preferred_element_type=jnp.float32)
    pre = pre + jnp.transpose(b_in, (1, 0, 2)).astype(jnp.float32)[:, None, :, :]
    hidden = jnp.tanh(pre).astype(jnp.bfloat16)
    pred = jnp.einsum("dnoh,nsdh->nos", w_out, hidden, preferred_element_type=jnp.float32)
    return pred + b_out[:, :, None]


def on_device(inputs, observed, noise, w_in, b_in, w_out, b_out):
    per_device = w_in.shape[0]
    f_in, hid = w_in.shape[1], w_in.shape[2]
    outs = w_out.shape[1]
    count = observed.shape[0] * lax.axis_size("member") * observed.shape[1] * lax.axis_size("dp")
    first = lax.axis_index("member") * per_device
    own = pack(w_in, b_in, w_out, b_out)
    whole = lax.all_gather(own, "member", axis=0, tiled=True)
    for update in range(UPDATES):
        own_b_out = own[:, -outs:]
        predicted = predict(inputs, own, own_b_out, f_in, hid, outs)
        collected = lax.all_to_all(predicted, "member", split_axis=1, concat_axis=0, tiled=True)
        mean_pred = jnp.mean(collected, axis=0)
        anomaly = (collected - mean_pred[None]).reshape(collected.shape[0], -1)
        misfit = (observed[None] + noise[update].astype(jnp.float32) - collected).reshape(
            collected.shape[0], -1
        )
        gram_part = lax.dot_general(
            anomaly, anomaly, (((1,), (1,)), ((), ())), precision=lax.Precision.HIGHEST
        )
        cross_part = lax.dot_general(
            anomaly, misfit, (((1,), (1,)), ((), ())), precision=lax.Precision.HIGHEST
        )
        gram, cross = lax.psum((gram_part, cross_part), ("member", "dp"))
        gain = solve_gain(gram / count, cross / count)
        if update + 1 < UPDATES:
            moved = lax.dot_general(
                gain, whole, (((0,), (0,)), ((), ())), precision=lax.Precision.HIGHEST
            )
            whole = whole + moved
            own = lax.dynamic_slice_in_dim(whole, first, per_device, 0)
        else:
            columns = lax.dynamic_slice_in_dim(gain, first, per_device, 1)
            moved = lax.dot_general(
                columns, whole, (((0,), (0,)), ((), ())), precision=lax.Precision.HIGHEST
            )
            own = own + moved
    return unpack(own, f_in, hid, outs)


def solution(mesh):
    placed = (
        P("dp", None),
        P("member", "dp"),
        P(None, None, "member", "dp"),
        P("member", None, "dp"),
        P("member", "dp"),
        P("member", None, "dp"),
        P("member", None),
    )
    return jax.shard_map(
        on_device,
        mesh=mesh,
        in_specs=placed,
        out_specs=(
            P("member", None, "dp"),
            P("member", "dp"),
            P("member", None, "dp"),
            P("member", None),
        ),
        check_vma=False,
    )
```

```python
import jax
import jax.numpy as jnp
from jax import lax
from jax.sharding import PartitionSpec as P

UPDATES = 2


ridge_level = 0.5


def solve_gain(gram, cross):
    eye = jnp.eye(gram.shape[0], dtype=gram.dtype)
    factor = jnp.linalg.cholesky(gram + ridge_level * eye)
    middle = lax.linalg.triangular_solve(factor, cross, left_side=True, lower=True)
    return lax.linalg.triangular_solve(factor, middle, left_side=True, lower=True, transpose_a=True)


def pack(w_in, b_in, w_out, b_out):
    n = w_in.shape[0]
    return jnp.concatenate(
        [w_in.reshape(n, -1), w_out.reshape(n, -1), b_in.reshape(n, -1), b_out.reshape(n, -1)], axis=1
    )


def unpack(flat, f_in, hid, outs):
    n = flat.shape[0]
    a = f_in * hid
    b = a + outs * hid
    c = b + hid
    return (
        flat[:, :a].reshape(n, f_in, hid),
        flat[:, b:c].reshape(n, hid),
        flat[:, a:b].reshape(n, outs, hid),
        flat[:, c:].reshape(n, outs),
    )


def gather_sum(x, axis):
    n = lax.axis_size(axis)
    tiles = jnp.broadcast_to(x[None], (n,) + x.shape)
    return jnp.sum(lax.all_to_all(tiles, axis, split_axis=0, concat_axis=0, tiled=True), axis=0)


def swap_pair(x):
    n = lax.axis_size("dp")
    return lax.ppermute(x, "dp", [(i, i ^ 1) for i in range(n)])


def predict(inputs_pair, own_flat, f_in, hid, outs, parity):
    n_dp = lax.axis_size("dp")
    a = f_in * hid
    b = a + outs * hid
    rounded = own_flat[:, : b + hid].astype(jnp.bfloat16)
    tiles = jnp.tile(rounded, (n_dp // rounded.shape[0], 1))
    got = lax.all_to_all(tiles, "dp", split_axis=0, concat_axis=0, tiled=True)
    d = got.shape[0]
    w_in = got[:, :a].reshape(d, f_in, hid)
    w_out = got[:, a:b].reshape(d, outs, hid)
    b_in = got[:, b : b + hid]
    b_out = jnp.where(parity == 0, own_flat[0, -outs:], own_flat[1, -outs:])
    pre = jnp.einsum("sf,dfh->sdh", inputs_pair, w_in, preferred_element_type=jnp.float32)
    pre = pre + b_in.astype(jnp.float32)[None]
    hidden = jnp.tanh(pre).astype(jnp.bfloat16)
    pred = jnp.einsum("doh,sdh->os", w_out, hidden, preferred_element_type=jnp.float32)
    return pred + b_out[:, None]


def collect(pred, n_samples, parity):
    n_m = lax.axis_size("member")
    outs = pred.shape[0]
    blocks = pred.reshape(n_m, outs // n_m, pred.shape[1])
    got = lax.all_to_all(blocks, "member", split_axis=0, concat_axis=0, tiled=True)
    mine = got[:, :, :n_samples]
    other = swap_pair(got[:, :, n_samples:])
    even = jnp.where(parity == 0, mine, other)
    odd = jnp.where(parity == 0, other, mine)
    return jnp.stack([even, odd], axis=1).reshape(2 * n_m, outs // n_m, n_samples)


def on_device(inputs, observed, noise, w_in, b_in, w_out, b_out):
    per_device = w_in.shape[0]
    f_in, hid = w_in.shape[1], w_in.shape[2]
    outs = w_out.shape[1]
    n_samples = inputs.shape[0]
    count = observed.shape[0] * lax.axis_size("member") * observed.shape[1] * lax.axis_size("dp")
    first = lax.axis_index("member") * per_device
    parity = lax.axis_index("dp") % 2
    inputs_pair = jnp.concatenate([inputs, swap_pair(inputs)], axis=0)
    own = pack(w_in, b_in, w_out, b_out)
    whole = lax.all_gather(own, "member", axis=0, tiled=True)
    for update in range(UPDATES):
        predicted = predict(inputs_pair, own, f_in, hid, outs, parity)
        collected = collect(predicted, n_samples, parity)
        mean_pred = jnp.mean(collected, axis=0)
        anomaly = (collected - mean_pred[None]).reshape(collected.shape[0], -1)
        misfit = (observed[None] + noise[update].astype(jnp.float32) - collected).reshape(
            collected.shape[0], -1
        )
        gram_part = lax.dot_general(
            anomaly, anomaly, (((1,), (1,)), ((), ())), precision=lax.Precision.HIGHEST
        )
        cross_part = lax.dot_general(
            anomaly, misfit, (((1,), (1,)), ((), ())), precision=lax.Precision.HIGHEST
        )
        sums = gather_sum(gather_sum(jnp.stack([gram_part, cross_part]), "member"), "dp")
        gain = solve_gain(sums[0] / count, sums[1] / count)
        if update + 1 < UPDATES:
            moved = lax.dot_general(
                gain, whole, (((0,), (0,)), ((), ())), precision=lax.Precision.HIGHEST
            )
            whole = whole + moved
            own = lax.dynamic_slice_in_dim(whole, first, per_device, 0)
        else:
            columns = lax.dynamic_slice_in_dim(gain, first, per_device, 1)
            moved = lax.dot_general(
                columns, whole, (((0,), (0,)), ((), ())), precision=lax.Precision.HIGHEST
            )
            own = own + moved
    return unpack(own, f_in, hid, outs)


def solution(mesh):
    placed = (
        P("dp", None),
        P("member", "dp"),
        P(None, None, "member", "dp"),
        P("member", None, "dp"),
        P("member", "dp"),
        P("member", None, "dp"),
        P("member", None),
    )
    return jax.shard_map(
        on_device,
        mesh=mesh,
        in_specs=placed,
        out_specs=(
            P("member", None, "dp"),
            P("member", "dp"),
            P("member", None, "dp"),
            P("member", None),
        ),
        check_vma=False,
    )
```

```python
import jax
import jax.numpy as jnp
from jax import lax
from jax.sharding import PartitionSpec as P

UPDATES = 2


ridge_level = 0.5


def solve_gain(gram, cross):
    eye = jnp.eye(gram.shape[0], dtype=gram.dtype)
    factor = jnp.linalg.cholesky(gram + ridge_level * eye)
    middle = lax.linalg.triangular_solve(factor, cross, left_side=True, lower=True)
    return lax.linalg.triangular_solve(factor, middle, left_side=True, lower=True, transpose_a=True)


def pack(w_in, b_in, w_out, b_out):
    n, hid = w_in.shape[0], w_in.shape[2]
    pad = jnp.zeros((n, hid - b_out.shape[1]), b_out.dtype)
    return jnp.concatenate(
        [w_in, w_out, b_in[:, None, :], jnp.concatenate([b_out, pad], axis=1)[:, None, :]], axis=1
    )


def unpack(flat, f_in, hid, outs):
    return (
        flat[:, :f_in, :],
        flat[:, f_in + outs, :],
        flat[:, f_in : f_in + outs, :],
        flat[:, f_in + outs + 1, :outs],
    )


def gather_sum(x, axis):
    n = lax.axis_size(axis)
    tiles = jnp.broadcast_to(x[None], (n,) + x.shape)
    return jnp.sum(lax.all_to_all(tiles, axis, split_axis=0, concat_axis=0, tiled=True), axis=0)


def swap_pair(x):
    n = lax.axis_size("dp")
    return lax.ppermute(x, "dp", [(i, i ^ 1) for i in range(n)])


def predict(inputs_pair, own_flat, f_in, hid, outs, parity):
    n_dp = lax.axis_size("dp")
    rows = f_in + outs + 1
    rounded = own_flat[:, :rows, :].astype(jnp.bfloat16)
    tiles = jnp.tile(rounded, (n_dp // rounded.shape[0], 1, 1))
    got = lax.all_to_all(tiles, "dp", split_axis=0, concat_axis=0, tiled=True)
    w_in = got[:, :f_in, :]
    w_out = got[:, f_in : f_in + outs, :]
    b_in = got[:, f_in + outs, :]
    b_out = jnp.where(parity == 0, own_flat[0, rows, :outs], own_flat[1, rows, :outs])
    pre = jnp.einsum("sf,dfh->sdh", inputs_pair, w_in, preferred_element_type=jnp.float32)
    pre = pre + b_in.astype(jnp.float32)[None]
    hidden = jnp.tanh(pre).astype(jnp.bfloat16)
    pred = jnp.einsum("doh,sdh->os", w_out, hidden, preferred_element_type=jnp.float32)
    return pred + b_out[:, None]


def collect(pred, n_samples, parity):
    n_m = lax.axis_size("member")
    outs = pred.shape[0]
    blocks = pred.reshape(n_m, outs // n_m, pred.shape[1])
    got = lax.all_to_all(blocks, "member", split_axis=0, concat_axis=0, tiled=True)
    mine = got[:, :, :n_samples]
    other = swap_pair(got[:, :, n_samples:])
    even = jnp.where(parity == 0, mine, other)
    odd = jnp.where(parity == 0, other, mine)
    return jnp.stack([even, odd], axis=1).reshape(2 * n_m, outs // n_m, n_samples)


def on_device(inputs, observed, noise, w_in, b_in, w_out, b_out):
    per_device = w_in.shape[0]
    f_in, hid = w_in.shape[1], w_in.shape[2]
    outs = w_out.shape[1]
    n_samples = inputs.shape[0]
    count = observed.shape[0] * lax.axis_size("member") * observed.shape[1] * lax.axis_size("dp")
    first = lax.axis_index("member") * per_device
    parity = lax.axis_index("dp") % 2
    inputs_pair = jnp.concatenate([inputs, swap_pair(inputs)], axis=0)
    own = pack(w_in, b_in, w_out, b_out)
    whole = lax.all_gather(own, "member", axis=0, tiled=True)
    for update in range(UPDATES):
        predicted = predict(inputs_pair, own, f_in, hid, outs, parity)
        collected = collect(predicted, n_samples, parity)
        mean_pred = jnp.mean(collected, axis=0)
        anomaly = (collected - mean_pred[None]).reshape(collected.shape[0], -1)
        misfit = (observed[None] + noise[update].astype(jnp.float32) - collected).reshape(
            collected.shape[0], -1
        )
        gram_part = lax.dot_general(
            anomaly, anomaly, (((1,), (1,)), ((), ())), precision=lax.Precision.HIGHEST
        )
        cross_part = lax.dot_general(
            anomaly, misfit, (((1,), (1,)), ((), ())), precision=lax.Precision.HIGHEST
        )
        sums = gather_sum(gather_sum(jnp.stack([gram_part, cross_part]), "member"), "dp")
        gain = solve_gain(sums[0] / count, sums[1] / count)
        if update + 1 < UPDATES:
            moved = jnp.einsum("kj,kab->jab", gain, whole, precision=lax.Precision.HIGHEST)
            whole = whole + moved
            own = lax.dynamic_slice_in_dim(whole, first, per_device, 0)
        else:
            columns = lax.dynamic_slice_in_dim(gain, first, per_device, 1)
            moved = jnp.einsum("kj,kab->jab", columns, whole, precision=lax.Precision.HIGHEST)
            own = own + moved
    return unpack(own, f_in, hid, outs)


def solution(mesh):
    placed = (
        P("dp", None),
        P("member", "dp"),
        P(None, None, "member", "dp"),
        P("member", None, "dp"),
        P("member", "dp"),
        P("member", None, "dp"),
        P("member", None),
    )
    return jax.shard_map(
        on_device,
        mesh=mesh,
        in_specs=placed,
        out_specs=(
            P("member", None, "dp"),
            P("member", "dp"),
            P("member", None, "dp"),
            P("member", None),
        ),
        check_vma=False,
    )
```

```python
import jax
import jax.numpy as jnp
from jax import lax
from jax.sharding import PartitionSpec as P

UPDATES = 2


ridge_level = 0.5


def solve_gain(gram, cross):
    eye = jnp.eye(gram.shape[0], dtype=gram.dtype)
    factor = jnp.linalg.cholesky(gram + ridge_level * eye)
    middle = lax.linalg.triangular_solve(factor, cross, left_side=True, lower=True)
    return lax.linalg.triangular_solve(factor, middle, left_side=True, lower=True, transpose_a=True)


def pack(w_in, b_in, w_out, b_out):
    n, hid = w_in.shape[0], w_in.shape[2]
    pad = jnp.zeros((n, hid - b_out.shape[1]), b_out.dtype)
    return jnp.concatenate(
        [w_in, w_out, b_in[:, None, :], jnp.concatenate([b_out, pad], axis=1)[:, None, :]], axis=1
    )


def unpack(flat, f_in, hid, outs):
    return (
        flat[:, :f_in, :],
        flat[:, f_in + outs, :],
        flat[:, f_in : f_in + outs, :],
        flat[:, f_in + outs + 1, :outs],
    )


def gather_sum(x, axis):
    n = lax.axis_size(axis)
    tiles = jnp.broadcast_to(x[None], (n,) + x.shape)
    return jnp.sum(lax.all_to_all(tiles, axis, split_axis=0, concat_axis=0, tiled=True), axis=0)


def swap_pair(x):
    n = lax.axis_size("dp")
    return lax.ppermute(x, "dp", [(i, i ^ 1) for i in range(n)])


def predict(inputs_pair, own_flat, f_in, hid, outs, parity):
    n_dp = lax.axis_size("dp")
    rows = f_in + outs + 1
    rounded = own_flat[:, :rows, :].astype(jnp.bfloat16)
    tiles = jnp.tile(rounded, (n_dp // rounded.shape[0], 1, 1))
    got = lax.all_to_all(tiles, "dp", split_axis=0, concat_axis=0, tiled=True)
    w_in = got[:, :f_in, :]
    w_out = got[:, f_in : f_in + outs, :]
    b_in = got[:, f_in + outs, :]
    b_out = jnp.where(parity == 0, own_flat[0, rows, :outs], own_flat[1, rows, :outs])
    pre = jnp.einsum("sf,dfh->sdh", inputs_pair, w_in, preferred_element_type=jnp.float32)
    pre = pre + b_in.astype(jnp.float32)[None]
    hidden = jnp.tanh(pre).astype(jnp.bfloat16)
    pred = jnp.einsum("doh,sdh->os", w_out, hidden, preferred_element_type=jnp.float32)
    return pred + b_out[:, None]


def collect(pred, n_samples, parity):
    n_m = lax.axis_size("member")
    outs = pred.shape[0]
    blocks = pred.reshape(n_m, outs // n_m, pred.shape[1])
    got = lax.all_to_all(blocks, "member", split_axis=0, concat_axis=0, tiled=True)
    mine = got[:, :, :n_samples]
    other = swap_pair(got[:, :, n_samples:])
    even = jnp.where(parity == 0, mine, other)
    odd = jnp.where(parity == 0, other, mine)
    return jnp.stack([even, odd], axis=1).reshape(2 * n_m, outs // n_m, n_samples)


def on_device(inputs, observed, noise, w_in, b_in, w_out, b_out):
    per_device = w_in.shape[0]
    f_in, hid = w_in.shape[1], w_in.shape[2]
    outs = w_out.shape[1]
    n_samples = inputs.shape[0]
    count = observed.shape[0] * lax.axis_size("member") * observed.shape[1] * lax.axis_size("dp")
    first = lax.axis_index("member") * per_device
    parity = lax.axis_index("dp") % 2
    inputs_pair = jnp.concatenate([inputs, swap_pair(inputs)], axis=0)
    own = pack(w_in, b_in, w_out, b_out)
    whole = lax.all_gather(own, "member", axis=0, tiled=True)
    for update in range(UPDATES):
        predicted = predict(inputs_pair, own, f_in, hid, outs, parity)
        collected = collect(predicted, n_samples, parity)
        mean_pred = jnp.mean(collected, axis=0)
        anomaly = (collected - mean_pred[None]).reshape(collected.shape[0], -1)
        misfit = (observed[None] + noise[update].astype(jnp.float32) - collected).reshape(
            collected.shape[0], -1
        )
        gram_part = lax.dot_general(
            anomaly, anomaly, (((1,), (1,)), ((), ())), precision=lax.Precision.HIGHEST
        )
        cross_part = lax.dot_general(
            anomaly, misfit, (((1,), (1,)), ((), ())), precision=lax.Precision.HIGHEST
        )
        sums = gather_sum(jnp.stack([gram_part, cross_part]), "member")
        if update == 0:
            sums = sums + whole[0, 0, 0] * 0
        sums = gather_sum(sums, "dp")
        gain = solve_gain(sums[0] / count, sums[1] / count)
        if update + 1 < UPDATES:
            moved = jnp.einsum("kj,kab->jab", gain, whole, precision=lax.Precision.HIGHEST)
            whole = whole + moved
            own = lax.dynamic_slice_in_dim(whole, first, per_device, 0)
        else:
            columns = lax.dynamic_slice_in_dim(gain, first, per_device, 1)
            moved = jnp.einsum("kj,kab->jab", columns, whole, precision=lax.Precision.HIGHEST)
            own = own + moved
    return unpack(own, f_in, hid, outs)


def solution(mesh):
    placed = (
        P("dp", None),
        P("member", "dp"),
        P(None, None, "member", "dp"),
        P("member", None, "dp"),
        P("member", "dp"),
        P("member", None, "dp"),
        P("member", None),
    )
    return jax.shard_map(
        on_device,
        mesh=mesh,
        in_specs=placed,
        out_specs=(
            P("member", None, "dp"),
            P("member", "dp"),
            P("member", None, "dp"),
            P("member", None),
        ),
        check_vma=False,
    )
```

```python
import jax
import jax.numpy as jnp
from jax import lax
from jax.sharding import PartitionSpec as P

UPDATES = 2


ridge_level = 0.5


def solve_gain(gram, cross):
    eye = jnp.eye(gram.shape[0], dtype=gram.dtype)
    factor = jnp.linalg.cholesky(gram + ridge_level * eye)
    middle = lax.linalg.triangular_solve(factor, cross, left_side=True, lower=True)
    return lax.linalg.triangular_solve(factor, middle, left_side=True, lower=True, transpose_a=True)


def pack(w_in, b_in, w_out, b_out):
    n, hid = w_in.shape[0], w_in.shape[2]
    pad = jnp.zeros((n, hid - b_out.shape[1]), b_out.dtype)
    return jnp.concatenate(
        [w_in, w_out, b_in[:, None, :], jnp.concatenate([b_out, pad], axis=1)[:, None, :]], axis=1
    )


def unpack(flat, f_in, hid, outs):
    return (
        flat[:, :f_in, :],
        flat[:, f_in + outs, :],
        flat[:, f_in : f_in + outs, :],
        flat[:, f_in + outs + 1, :outs],
    )


def gather_sum(x, axis):
    n = lax.axis_size(axis)
    tiles = jnp.broadcast_to(x[None], (n,) + x.shape)
    return jnp.sum(lax.all_to_all(tiles, axis, split_axis=0, concat_axis=0, tiled=True), axis=0)


def swap_pair(x):
    n = lax.axis_size("dp")
    return lax.ppermute(x, "dp", [(i, i ^ 1) for i in range(n)])


def predict(inputs_pair, own_flat, f_in, hid, outs, parity):
    n_dp = lax.axis_size("dp")
    rows = f_in + outs + 1
    rounded = own_flat[:, :rows, :].astype(jnp.bfloat16)
    n = rounded.shape[0]
    tiles = jnp.broadcast_to(rounded[None], (n_dp // n,) + rounded.shape).reshape((n_dp,) + rounded.shape[1:])
    got = lax.all_to_all(tiles, "dp", split_axis=0, concat_axis=0, tiled=True)
    w_in = got[:, :f_in, :]
    w_out = got[:, f_in : f_in + outs, :]
    b_in = got[:, f_in + outs, :]
    b_out = jnp.where(parity == 0, own_flat[0, rows, :outs], own_flat[1, rows, :outs])
    pre = jnp.einsum("sf,dfh->sdh", inputs_pair, w_in, preferred_element_type=jnp.float32)
    pre = pre + b_in.astype(jnp.float32)[None]
    hidden = jnp.tanh(pre).astype(jnp.bfloat16)
    pred = jnp.einsum("doh,sdh->os", w_out, hidden, preferred_element_type=jnp.float32)
    return pred + b_out[:, None]


def collect(pred, n_samples, parity):
    n_m = lax.axis_size("member")
    outs = pred.shape[0]
    blocks = pred.reshape(n_m, outs // n_m, pred.shape[1])
    got = lax.all_to_all(blocks, "member", split_axis=0, concat_axis=0, tiled=True)
    mine = got[:, :, :n_samples]
    other = swap_pair(got[:, :, n_samples:])
    even = jnp.where(parity == 0, mine, other)
    odd = jnp.where(parity == 0, other, mine)
    return jnp.stack([even, odd], axis=1).reshape(2 * n_m, outs // n_m, n_samples)


def on_device(inputs, observed, noise, w_in, b_in, w_out, b_out):
    per_device = w_in.shape[0]
    f_in, hid = w_in.shape[1], w_in.shape[2]
    outs = w_out.shape[1]
    n_samples = inputs.shape[0]
    count = observed.shape[0] * lax.axis_size("member") * observed.shape[1] * lax.axis_size("dp")
    first = lax.axis_index("member") * per_device
    parity = lax.axis_index("dp") % 2
    inputs_pair = jnp.concatenate([inputs, swap_pair(inputs)], axis=0)
    own = pack(w_in, b_in, w_out, b_out)
    whole = lax.all_gather(own, "member", axis=0, tiled=True)
    assert UPDATES == 2
    for update in range(UPDATES):
        predicted = predict(inputs_pair, own, f_in, hid, outs, parity)
        collected = collect(predicted, n_samples, parity)
        mean_pred = jnp.mean(collected, axis=0)
        anomaly = (collected - mean_pred[None]).reshape(collected.shape[0], -1)
        misfit = (observed[None] + noise[update].astype(jnp.float32) - collected).reshape(
            collected.shape[0], -1
        )
        gram_part = lax.dot_general(
            anomaly, anomaly, (((1,), (1,)), ((), ())), precision=lax.Precision.HIGHEST
        )
        cross_part = lax.dot_general(
            anomaly, misfit, (((1,), (1,)), ((), ())), precision=lax.Precision.HIGHEST
        )
        sums = gather_sum(jnp.stack([gram_part, cross_part]), "member")
        if update == 0:
            sums = sums + whole[0, 0, 0] * 0
        sums = gather_sum(sums, "dp")
        gain = solve_gain(sums[0] / count, sums[1] / count)
        if update == 0:
            first_gain = gain
            columns = lax.dynamic_slice_in_dim(gain, first, per_device, 1)
            own = own + jnp.einsum("kj,kab->jab", columns, whole, precision=lax.Precision.HIGHEST)
        else:
            eye = jnp.eye(gain.shape[0], dtype=gain.dtype)
            through = jnp.dot(eye + first_gain, gain, precision=lax.Precision.HIGHEST)
            columns = lax.dynamic_slice_in_dim(through, first, per_device, 1)
            own = own + jnp.einsum("kj,kab->jab", columns, whole, precision=lax.Precision.HIGHEST)
    return unpack(own, f_in, hid, outs)


def solution(mesh):
    placed = (
        P("dp", None),
        P("member", "dp"),
        P(None, None, "member", "dp"),
        P("member", None, "dp"),
        P("member", "dp"),
        P("member", None, "dp"),
        P("member", None),
    )
    return jax.shard_map(
        on_device,
        mesh=mesh,
        in_specs=placed,
        out_specs=(
            P("member", None, "dp"),
            P("member", "dp"),
            P("member", None, "dp"),
            P("member", None),
        ),
        check_vma=False,
    )
```

```python
import jax
import jax.numpy as jnp
from jax import lax
from jax.experimental import pallas as pl
from jax.sharding import PartitionSpec as P

UPDATES = 2


ridge_level = 0.5


def solve_gain(gram, cross):
    eye = jnp.eye(gram.shape[0], dtype=gram.dtype)
    factor = jnp.linalg.cholesky(gram + ridge_level * eye)
    middle = lax.linalg.triangular_solve(factor, cross, left_side=True, lower=True)
    return lax.linalg.triangular_solve(factor, middle, left_side=True, lower=True, transpose_a=True)


def _eliminate(a_ref, b_ref, o_ref):
    n = a_ref.shape[0]
    a = a_ref[...]
    b = b_ref[...]
    rows = lax.broadcasted_iota(jnp.int32, a.shape, 0)
    cols = lax.broadcasted_iota(jnp.int32, a.shape, 1)
    rows_b = lax.broadcasted_iota(jnp.int32, b.shape, 0)

    def step(k, carry):
        a, b = carry
        row_a = jnp.sum(jnp.where(rows == k, a, 0.0), axis=0, keepdims=True)
        row_b = jnp.sum(jnp.where(rows_b == k, b, 0.0), axis=0, keepdims=True)
        col = jnp.sum(jnp.where(cols == k, a, 0.0), axis=1, keepdims=True)
        pivot = jnp.sum(jnp.where(cols[:1] == k, row_a, 0.0), axis=1, keepdims=True)
        ra = row_a / pivot
        rb = row_b / pivot
        a = jnp.where(rows == k, ra, a - col * ra)
        b = jnp.where(rows_b == k, rb, b - col * rb)
        return a, b

    a, b = lax.fori_loop(0, n, step, (a, b))
    o_ref[...] = b

def solve_spd(a, b):
    return pl.pallas_call(_eliminate, out_shape=jax.ShapeDtypeStruct(b.shape, b.dtype))(a, b)

def pack(w_in, b_in, w_out, b_out):
    n, hid = w_in.shape[0], w_in.shape[2]
    pad = jnp.zeros((n, hid - b_out.shape[1]), b_out.dtype)
    return jnp.concatenate(
        [w_in, w_out, b_in[:, None, :], jnp.concatenate([b_out, pad], axis=1)[:, None, :]], axis=1
    )


def unpack(flat, f_in, hid, outs):
    return (
        flat[:, :f_in, :],
        flat[:, f_in + outs, :],
        flat[:, f_in : f_in + outs, :],
        flat[:, f_in + outs + 1, :outs],
    )


def gather_sum(x, axis):
    n = lax.axis_size(axis)
    tiles = jnp.broadcast_to(x[None], (n,) + x.shape)
    return jnp.sum(lax.all_to_all(tiles, axis, split_axis=0, concat_axis=0, tiled=True), axis=0)


def swap_pair(x):
    n = lax.axis_size("dp")
    return lax.ppermute(x, "dp", [(i, i ^ 1) for i in range(n)])


def predict(inputs_pair, own_flat, f_in, hid, outs, parity):
    n_dp = lax.axis_size("dp")
    rows = f_in + outs + 1
    rounded = own_flat[:, :rows, :].astype(jnp.bfloat16)
    n = rounded.shape[0]
    tiles = jnp.broadcast_to(rounded[None], (n_dp // n,) + rounded.shape).reshape((n_dp,) + rounded.shape[1:])
    got = lax.all_to_all(tiles, "dp", split_axis=0, concat_axis=0, tiled=True)
    w_in = got[:, :f_in, :]
    w_out = got[:, f_in : f_in + outs, :]
    b_in = got[:, f_in + outs, :]
    b_out = jnp.where(parity == 0, own_flat[0, rows, :outs], own_flat[1, rows, :outs])
    pre = jnp.einsum("sf,dfh->sdh", inputs_pair, w_in, preferred_element_type=jnp.float32)
    pre = pre + b_in.astype(jnp.float32)[None]
    hidden = jnp.tanh(pre).astype(jnp.bfloat16)
    pred = jnp.einsum("doh,sdh->os", w_out, hidden, preferred_element_type=jnp.float32)
    return pred + b_out[:, None]


def collect(pred, n_samples, parity):
    n_m = lax.axis_size("member")
    outs = pred.shape[0]
    blocks = pred.reshape(n_m, outs // n_m, pred.shape[1])
    got = lax.all_to_all(blocks, "member", split_axis=0, concat_axis=0, tiled=True)
    mine = got[:, :, :n_samples]
    other = swap_pair(got[:, :, n_samples:])
    even = jnp.where(parity == 0, mine, other)
    odd = jnp.where(parity == 0, other, mine)
    return jnp.stack([even, odd], axis=1).reshape(2 * n_m, outs // n_m, n_samples)


def on_device(inputs, observed, noise, w_in, b_in, w_out, b_out):
    per_device = w_in.shape[0]
    f_in, hid = w_in.shape[1], w_in.shape[2]
    outs = w_out.shape[1]
    n_samples = inputs.shape[0]
    count = observed.shape[0] * lax.axis_size("member") * observed.shape[1] * lax.axis_size("dp")
    first = lax.axis_index("member") * per_device
    parity = lax.axis_index("dp") % 2
    inputs_pair = jnp.concatenate([inputs, swap_pair(inputs)], axis=0)
    own = pack(w_in, b_in, w_out, b_out)
    whole = lax.all_gather(own, "member", axis=0, tiled=True)
    assert UPDATES == 2
    for update in range(UPDATES):
        predicted = predict(inputs_pair, own, f_in, hid, outs, parity)
        collected = collect(predicted, n_samples, parity)
        mean_pred = jnp.mean(collected, axis=0)
        anomaly = (collected - mean_pred[None]).reshape(collected.shape[0], -1)
        misfit = (observed[None] + noise[update].astype(jnp.float32) - collected).reshape(
            collected.shape[0], -1
        )
        gram_part = lax.dot_general(
            anomaly, anomaly, (((1,), (1,)), ((), ())), precision=lax.Precision.HIGHEST
        )
        cross_part = lax.dot_general(
            anomaly, misfit, (((1,), (1,)), ((), ())), precision=lax.Precision.HIGHEST
        )
        sums = gather_sum(jnp.stack([gram_part, cross_part]), "member")
        if update == 0:
            sums = sums + whole[0, 0, 0] * 0
        sums = gather_sum(sums, "dp")
        eye = jnp.eye(sums.shape[1], dtype=sums.dtype)
        gain = solve_spd(sums[0] / count + ridge_level * eye, sums[1] / count)
        if update == 0:
            first_gain = gain
            columns = lax.dynamic_slice_in_dim(gain, first, per_device, 1)
            own = own + jnp.einsum("kj,kab->jab", columns, whole, precision=lax.Precision.HIGHEST)
        else:
            eye = jnp.eye(gain.shape[0], dtype=gain.dtype)
            through = jnp.dot(eye + first_gain, gain, precision=lax.Precision.HIGHEST)
            columns = lax.dynamic_slice_in_dim(through, first, per_device, 1)
            own = own + jnp.einsum("kj,kab->jab", columns, whole, precision=lax.Precision.HIGHEST)
    return unpack(own, f_in, hid, outs)


def solution(mesh):
    placed = (
        P("dp", None),
        P("member", "dp"),
        P(None, None, "member", "dp"),
        P("member", None, "dp"),
        P("member", "dp"),
        P("member", None, "dp"),
        P("member", None),
    )
    return jax.shard_map(
        on_device,
        mesh=mesh,
        in_specs=placed,
        out_specs=(
            P("member", None, "dp"),
            P("member", "dp"),
            P("member", None, "dp"),
            P("member", None),
        ),
        check_vma=False,
    )
```

```python
import jax
import jax.numpy as jnp
from jax import lax
from jax.experimental import pallas as pl
from jax.sharding import PartitionSpec as P

UPDATES = 2


ridge_level = 0.5


def solve_gain(gram, cross):
    eye = jnp.eye(gram.shape[0], dtype=gram.dtype)
    factor = jnp.linalg.cholesky(gram + ridge_level * eye)
    middle = lax.linalg.triangular_solve(factor, cross, left_side=True, lower=True)
    return lax.linalg.triangular_solve(factor, middle, left_side=True, lower=True, transpose_a=True)


def _eliminate(a_ref, b_ref, o_ref):
    n = a_ref.shape[0]
    a = a_ref[...]
    b = b_ref[...]
    rows = lax.broadcasted_iota(jnp.int32, a.shape, 0)
    cols = lax.broadcasted_iota(jnp.int32, a.shape, 1)
    rows_b = lax.broadcasted_iota(jnp.int32, b.shape, 0)

    def step(k, carry):
        a, b = carry
        row_a = jnp.sum(jnp.where(rows == k, a, 0.0), axis=0, keepdims=True)
        row_b = jnp.sum(jnp.where(rows_b == k, b, 0.0), axis=0, keepdims=True)
        col = jnp.sum(jnp.where(cols == k, a, 0.0), axis=1, keepdims=True)
        pivot = jnp.sum(jnp.where(cols[:1] == k, row_a, 0.0), axis=1, keepdims=True)
        ra = row_a / pivot
        rb = row_b / pivot
        a = jnp.where(rows == k, ra, a - col * ra)
        b = jnp.where(rows_b == k, rb, b - col * rb)
        return a, b

    a, b = lax.fori_loop(0, n, step, (a, b), unroll=True)
    o_ref[...] = b

def solve_spd(a, b):
    return pl.pallas_call(_eliminate, out_shape=jax.ShapeDtypeStruct(b.shape, b.dtype))(a, b)

def pack(w_in, b_in, w_out, b_out):
    n, hid = w_in.shape[0], w_in.shape[2]
    pad = jnp.zeros((n, hid - b_out.shape[1]), b_out.dtype)
    return jnp.concatenate(
        [w_in, w_out, b_in[:, None, :], jnp.concatenate([b_out, pad], axis=1)[:, None, :]], axis=1
    )


def unpack(flat, f_in, hid, outs):
    return (
        flat[:, :f_in, :],
        flat[:, f_in + outs, :],
        flat[:, f_in : f_in + outs, :],
        flat[:, f_in + outs + 1, :outs],
    )


def gather_sum(x, axis):
    n = lax.axis_size(axis)
    tiles = jnp.broadcast_to(x[None], (n,) + x.shape)
    return jnp.sum(lax.all_to_all(tiles, axis, split_axis=0, concat_axis=0, tiled=True), axis=0)


def swap_pair(x):
    n = lax.axis_size("dp")
    return lax.ppermute(x, "dp", [(i, i ^ 1) for i in range(n)])


def predict(inputs_pair, own_flat, f_in, hid, outs, parity):
    n_dp = lax.axis_size("dp")
    rows = f_in + outs + 1
    rounded = own_flat[:, :rows, :].astype(jnp.bfloat16)
    n = rounded.shape[0]
    tiles = jnp.broadcast_to(rounded[None], (n_dp // n,) + rounded.shape).reshape((n_dp,) + rounded.shape[1:])
    got = lax.all_to_all(tiles, "dp", split_axis=0, concat_axis=0, tiled=True)
    w_in = got[:, :f_in, :]
    w_out = got[:, f_in : f_in + outs, :]
    b_in = got[:, f_in + outs, :]
    b_out = jnp.where(parity == 0, own_flat[0, rows, :outs], own_flat[1, rows, :outs])
    pre = jnp.einsum("sf,dfh->sdh", inputs_pair, w_in, preferred_element_type=jnp.float32)
    pre = pre + b_in.astype(jnp.float32)[None]
    hidden = jnp.tanh(pre).astype(jnp.bfloat16)
    pred = jnp.einsum("doh,sdh->os", w_out, hidden, preferred_element_type=jnp.float32)
    return pred + b_out[:, None]


def collect(pred, n_samples, parity):
    n_m = lax.axis_size("member")
    outs = pred.shape[0]
    blocks = pred.reshape(n_m, outs // n_m, pred.shape[1])
    got = lax.all_to_all(blocks, "member", split_axis=0, concat_axis=0, tiled=True)
    mine = got[:, :, :n_samples]
    other = swap_pair(got[:, :, n_samples:])
    even = jnp.where(parity == 0, mine, other)
    odd = jnp.where(parity == 0, other, mine)
    return jnp.stack([even, odd], axis=1).reshape(2 * n_m, outs // n_m, n_samples)


def on_device(inputs, observed, noise, w_in, b_in, w_out, b_out):
    per_device = w_in.shape[0]
    f_in, hid = w_in.shape[1], w_in.shape[2]
    outs = w_out.shape[1]
    n_samples = inputs.shape[0]
    count = observed.shape[0] * lax.axis_size("member") * observed.shape[1] * lax.axis_size("dp")
    first = lax.axis_index("member") * per_device
    parity = lax.axis_index("dp") % 2
    inputs_pair = jnp.concatenate([inputs, swap_pair(inputs)], axis=0)
    own = pack(w_in, b_in, w_out, b_out)
    whole = lax.all_gather(own, "member", axis=0, tiled=True)
    assert UPDATES == 2
    for update in range(UPDATES):
        predicted = predict(inputs_pair, own, f_in, hid, outs, parity)
        collected = collect(predicted, n_samples, parity)
        mean_pred = jnp.mean(collected, axis=0)
        anomaly = (collected - mean_pred[None]).reshape(collected.shape[0], -1)
        misfit = (observed[None] + noise[update].astype(jnp.float32) - collected).reshape(
            collected.shape[0], -1
        )
        gram_part = lax.dot_general(
            anomaly, anomaly, (((1,), (1,)), ((), ())), precision=lax.Precision.HIGHEST
        )
        cross_part = lax.dot_general(
            anomaly, misfit, (((1,), (1,)), ((), ())), precision=lax.Precision.HIGHEST
        )
        sums = gather_sum(gather_sum(jnp.stack([gram_part, cross_part]), "member"), "dp")
        if update == 0:
            sums = sums + whole[0, 0, 0] * 0
        eye = jnp.eye(sums.shape[1], dtype=sums.dtype)
        gain = solve_spd(sums[0] / count + ridge_level * eye, sums[1] / count)
        if update == 0:
            first_gain = gain
            columns = lax.dynamic_slice_in_dim(gain, first, per_device, 1)
            own = own + jnp.einsum("kj,kab->jab", columns, whole, precision=lax.Precision.HIGH)
        else:
            eye = jnp.eye(gain.shape[0], dtype=gain.dtype)
            through = jnp.dot(eye + first_gain, gain, precision=lax.Precision.HIGHEST)
            columns = lax.dynamic_slice_in_dim(through, first, per_device, 1)
            own = own + jnp.einsum("kj,kab->jab", columns, whole, precision=lax.Precision.HIGH)
    return unpack(own, f_in, hid, outs)


def solution(mesh):
    placed = (
        P("dp", None),
        P("member", "dp"),
        P(None, None, "member", "dp"),
        P("member", None, "dp"),
        P("member", "dp"),
        P("member", None, "dp"),
        P("member", None),
    )
    return jax.shard_map(
        on_device,
        mesh=mesh,
        in_specs=placed,
        out_specs=(
            P("member", None, "dp"),
            P("member", "dp"),
            P("member", None, "dp"),
            P("member", None),
        ),
        check_vma=False,
    )
```

```python
import jax
import jax.numpy as jnp
from jax import lax
from jax.experimental import pallas as pl
from jax.sharding import PartitionSpec as P

UPDATES = 2


ridge_level = 0.5


def solve_gain(gram, cross):
    eye = jnp.eye(gram.shape[0], dtype=gram.dtype)
    factor = jnp.linalg.cholesky(gram + ridge_level * eye)
    middle = lax.linalg.triangular_solve(factor, cross, left_side=True, lower=True)
    return lax.linalg.triangular_solve(factor, middle, left_side=True, lower=True, transpose_a=True)


def _eliminate(a_ref, b_ref, o_ref):
    n = a_ref.shape[0]
    a = a_ref[...]
    b = b_ref[...]
    rows = lax.broadcasted_iota(jnp.int32, a.shape, 0)
    cols = lax.broadcasted_iota(jnp.int32, a.shape, 1)
    rows_b = lax.broadcasted_iota(jnp.int32, b.shape, 0)

    def step(k, carry):
        a, b = carry
        row_a = jnp.sum(jnp.where(rows == k, a, 0.0), axis=0, keepdims=True)
        row_b = jnp.sum(jnp.where(rows_b == k, b, 0.0), axis=0, keepdims=True)
        col = jnp.sum(jnp.where(cols == k, a, 0.0), axis=1, keepdims=True)
        pivot = jnp.sum(jnp.where(cols[:1] == k, row_a, 0.0), axis=1, keepdims=True)
        ra = row_a / pivot
        rb = row_b / pivot
        a = jnp.where(rows == k, ra, a - col * ra)
        b = jnp.where(rows_b == k, rb, b - col * rb)
        return a, b

    a, b = lax.fori_loop(0, n, step, (a, b), unroll=True)
    o_ref[...] = b

def solve_spd(a, b):
    return pl.pallas_call(_eliminate, out_shape=jax.ShapeDtypeStruct(b.shape, b.dtype))(a, b)

def pack(w_in, b_in, w_out, b_out):
    n, hid = w_in.shape[0], w_in.shape[2]
    pad = jnp.zeros((n, hid - b_out.shape[1]), b_out.dtype)
    return jnp.concatenate(
        [w_in, w_out, b_in[:, None, :], jnp.concatenate([b_out, pad], axis=1)[:, None, :]], axis=1
    )


def unpack(flat, f_in, hid, outs):
    return (
        flat[:, :f_in, :],
        flat[:, f_in + outs, :],
        flat[:, f_in : f_in + outs, :],
        flat[:, f_in + outs + 1, :outs],
    )


def gather_sum(x, axis):
    n = lax.axis_size(axis)
    flat = x.reshape(-1, 128)
    tiles = jnp.broadcast_to(flat[None], (n,) + flat.shape)
    got = lax.all_to_all(tiles, axis, split_axis=0, concat_axis=0, tiled=True)
    return jnp.sum(got, axis=0).reshape(x.shape)


def swap_pair(x):
    n = lax.axis_size("dp")
    return lax.ppermute(x, "dp", [(i, i ^ 1) for i in range(n)])


def predict(inputs_pair, own_flat, f_in, hid, outs, parity):
    n_dp = lax.axis_size("dp")
    rows = f_in + outs + 1
    rounded = own_flat[:, :rows, :].astype(jnp.bfloat16)
    n = rounded.shape[0]
    tiles = jnp.broadcast_to(rounded[None], (n_dp // n,) + rounded.shape).reshape((n_dp,) + rounded.shape[1:])
    got = lax.all_to_all(tiles, "dp", split_axis=0, concat_axis=0, tiled=True)
    w_in = got[:, :f_in, :]
    w_out = got[:, f_in : f_in + outs, :]
    b_in = got[:, f_in + outs, :]
    b_out = jnp.where(parity == 0, own_flat[0, rows, :outs], own_flat[1, rows, :outs])
    pre = jnp.einsum("sf,dfh->sdh", inputs_pair, w_in, preferred_element_type=jnp.float32)
    pre = pre + b_in.astype(jnp.float32)[None]
    hidden = jnp.tanh(pre).astype(jnp.bfloat16)
    pred = jnp.einsum("doh,sdh->os", w_out, hidden, preferred_element_type=jnp.float32)
    return pred + b_out[:, None]


def collect(pred, n_samples, parity):
    n_m = lax.axis_size("member")
    outs = pred.shape[0]
    blocks = pred.reshape(n_m, outs // n_m, pred.shape[1])
    got = lax.all_to_all(blocks, "member", split_axis=0, concat_axis=0, tiled=True)
    mine = got[:, :, :n_samples]
    other = swap_pair(got[:, :, n_samples:])
    even = jnp.where(parity == 0, mine, other)
    odd = jnp.where(parity == 0, other, mine)
    return jnp.stack([even, odd], axis=1).reshape(2 * n_m, outs // n_m, n_samples)


def on_device(inputs, observed, noise, w_in, b_in, w_out, b_out):
    per_device = w_in.shape[0]
    f_in, hid = w_in.shape[1], w_in.shape[2]
    outs = w_out.shape[1]
    n_samples = inputs.shape[0]
    count = observed.shape[0] * lax.axis_size("member") * observed.shape[1] * lax.axis_size("dp")
    first = lax.axis_index("member") * per_device
    parity = lax.axis_index("dp") % 2
    inputs_pair = jnp.concatenate([inputs, swap_pair(inputs)], axis=0)
    own = pack(w_in, b_in, w_out, b_out)
    whole = lax.all_gather(own, "member", axis=0, tiled=True)
    assert UPDATES == 2
    for update in range(UPDATES):
        predicted = predict(inputs_pair, own, f_in, hid, outs, parity)
        collected = collect(predicted, n_samples, parity)
        mean_pred = jnp.mean(collected, axis=0)
        anomaly = (collected - mean_pred[None]).reshape(collected.shape[0], -1)
        misfit = (observed[None] + noise[update].astype(jnp.float32) - collected).reshape(
            collected.shape[0], -1
        )
        gram_part = lax.dot_general(
            anomaly, anomaly, (((1,), (1,)), ((), ())), precision=lax.Precision.HIGHEST
        )
        cross_part = lax.dot_general(
            anomaly, misfit, (((1,), (1,)), ((), ())), precision=lax.Precision.HIGHEST
        )
        sums = gather_sum(gather_sum(jnp.stack([gram_part, cross_part]), "member"), "dp")
        if update == 0:
            sums = sums + whole[0, 0, 0] * 0
        eye = jnp.eye(sums.shape[1], dtype=sums.dtype)
        gain = solve_spd(sums[0] / count + ridge_level * eye, sums[1] / count)
        if update == 0:
            first_gain = gain
            columns = lax.dynamic_slice_in_dim(gain, first, per_device, 1)
            own = own + jnp.einsum("kj,kab->jab", columns, whole, precision=lax.Precision.HIGH)
        else:
            eye = jnp.eye(gain.shape[0], dtype=gain.dtype)
            through = jnp.dot(eye + first_gain, gain, precision=lax.Precision.HIGHEST)
            columns = lax.dynamic_slice_in_dim(through, first, per_device, 1)

            def part(rows, cut=None):
                base, src = own[:, rows], whole[:, rows]
                if cut is not None:
                    base, src = base[..., :cut], src[..., :cut]
                return base + jnp.einsum("kj,k...->j...", columns, src, precision=lax.Precision.HIGH)

            return (
                part(slice(0, f_in)),
                part(f_in + outs),
                part(slice(f_in, f_in + outs)),
                part(f_in + outs + 1, outs),
            )
    return unpack(own, f_in, hid, outs)


def solution(mesh):
    placed = (
        P("dp", None),
        P("member", "dp"),
        P(None, None, "member", "dp"),
        P("member", None, "dp"),
        P("member", "dp"),
        P("member", None, "dp"),
        P("member", None),
    )
    return jax.shard_map(
        on_device,
        mesh=mesh,
        in_specs=placed,
        out_specs=(
            P("member", None, "dp"),
            P("member", "dp"),
            P("member", None, "dp"),
            P("member", None),
        ),
        check_vma=False,
    )
```

```python
import functools

import jax
import jax.numpy as jnp
from jax import lax
from jax.experimental import pallas as pl
from jax.sharding import PartitionSpec as P

UPDATES = 2


ridge_level = 0.5


def solve_gain(gram, cross):
    eye = jnp.eye(gram.shape[0], dtype=gram.dtype)
    factor = jnp.linalg.cholesky(gram + ridge_level * eye)
    middle = lax.linalg.triangular_solve(factor, cross, left_side=True, lower=True)
    return lax.linalg.triangular_solve(factor, middle, left_side=True, lower=True, transpose_a=True)


def _eliminate(s_ref, o_ref, *, scale, ridge):
    a = s_ref[0] * scale
    b = s_ref[1] * scale
    n = a.shape[0]
    rows = lax.broadcasted_iota(jnp.int32, a.shape, 0)
    cols = lax.broadcasted_iota(jnp.int32, a.shape, 1)
    a = jnp.where(rows == cols, a + ridge, a)
    for k in range(n):
        pivot = a[k : k + 1, k : k + 1]
        ra = a[k : k + 1, :] / pivot
        rb = b[k : k + 1, :] / pivot
        col = a[:, k : k + 1]
        a = jnp.where(rows == k, ra, a - col * ra)
        b = jnp.where(rows == k, rb, b - col * rb)
    o_ref[...] = b

def solve_spd(sums, scale, ridge):
    kernel = functools.partial(_eliminate, scale=scale, ridge=ridge)
    return pl.pallas_call(kernel, out_shape=jax.ShapeDtypeStruct(sums.shape[1:], sums.dtype))(sums)

def pack(w_in, b_in, w_out, b_out):
    n, hid = w_in.shape[0], w_in.shape[2]
    pad = jnp.zeros((n, hid - b_out.shape[1]), b_out.dtype)
    return jnp.concatenate(
        [w_in, w_out, b_in[:, None, :], jnp.concatenate([b_out, pad], axis=1)[:, None, :]], axis=1
    )


def unpack(flat, f_in, hid, outs):
    return (
        flat[:, :f_in, :],
        flat[:, f_in + outs, :],
        flat[:, f_in : f_in + outs, :],
        flat[:, f_in + outs + 1, :outs],
    )


def gather_sum(x, axis):
    n = lax.axis_size(axis)
    flat = x.reshape(-1, 128)
    tiles = jnp.broadcast_to(flat[None], (n,) + flat.shape)
    got = lax.all_to_all(tiles, axis, split_axis=0, concat_axis=0, tiled=True)
    return jnp.sum(got, axis=0).reshape(x.shape)


def swap_pair(x):
    n = lax.axis_size("dp")
    return lax.ppermute(x, "dp", [(i, i ^ 1) for i in range(n)])


def predict(inputs_pair, own_flat, f_in, hid, outs, parity):
    n_dp = lax.axis_size("dp")
    rows = f_in + outs + 1
    rounded = own_flat[:, :rows, :].astype(jnp.bfloat16)
    n = rounded.shape[0]
    tiles = jnp.broadcast_to(rounded[None], (n_dp // n,) + rounded.shape).reshape((n_dp,) + rounded.shape[1:])
    got = lax.all_to_all(tiles, "dp", split_axis=0, concat_axis=0, tiled=True)
    w_in = got[:, :f_in, :]
    w_out = got[:, f_in : f_in + outs, :]
    b_in = got[:, f_in + outs, :]
    b_out = jnp.where(parity == 0, own_flat[0, rows, :outs], own_flat[1, rows, :outs])
    pre = jnp.einsum("sf,dfh->sdh", inputs_pair, w_in, preferred_element_type=jnp.float32)
    pre = pre + b_in.astype(jnp.float32)[None]
    hidden = jnp.tanh(pre).astype(jnp.bfloat16)
    pred = jnp.einsum("doh,sdh->os", w_out, hidden, preferred_element_type=jnp.float32)
    return pred + b_out[:, None]


def collect(pred, n_samples, parity):
    n_m = lax.axis_size("member")
    outs = pred.shape[0]
    blocks = pred.reshape(n_m, outs // n_m, pred.shape[1])
    got = lax.all_to_all(blocks, "member", split_axis=0, concat_axis=0, tiled=True)
    mine = got[:, :, :n_samples]
    other = swap_pair(got[:, :, n_samples:])
    even = jnp.where(parity == 0, mine, other)
    odd = jnp.where(parity == 0, other, mine)
    return jnp.stack([even, odd], axis=1).reshape(2 * n_m, outs // n_m, n_samples)


def on_device(inputs, observed, noise, w_in, b_in, w_out, b_out):
    per_device = w_in.shape[0]
    f_in, hid = w_in.shape[1], w_in.shape[2]
    outs = w_out.shape[1]
    n_samples = inputs.shape[0]
    count = observed.shape[0] * lax.axis_size("member") * observed.shape[1] * lax.axis_size("dp")
    first = lax.axis_index("member") * per_device
    parity = lax.axis_index("dp") % 2
    inputs_pair = jnp.concatenate([inputs, swap_pair(inputs)], axis=0)
    own = pack(w_in, b_in, w_out, b_out)
    whole = lax.all_gather(own, "member", axis=0, tiled=True)
    assert UPDATES == 2
    for update in range(UPDATES):
        predicted = predict(inputs_pair, own, f_in, hid, outs, parity)
        collected = collect(predicted, n_samples, parity)
        mean_pred = jnp.mean(collected, axis=0)
        anomaly = (collected - mean_pred[None]).reshape(collected.shape[0], -1)
        misfit = (observed[None] + noise[update].astype(jnp.float32) - collected).reshape(
            collected.shape[0], -1
        )
        gram_part = lax.dot_general(
            anomaly, anomaly, (((1,), (1,)), ((), ())), precision=lax.Precision.HIGHEST
        )
        cross_part = lax.dot_general(
            anomaly, misfit, (((1,), (1,)), ((), ())), precision=lax.Precision.HIGHEST
        )
        sums = gather_sum(gather_sum(jnp.stack([gram_part, cross_part]), "member"), "dp")
        if update == 0:
            sums = sums + whole[0, 0, 0] * 0
        gain = solve_spd(sums, 1.0 / count, ridge_level)
        if update == 0:
            first_gain = gain
            columns = lax.dynamic_slice_in_dim(gain, first, per_device, 1)
            own = own + jnp.einsum("kj,kab->jab", columns, whole, precision=lax.Precision.HIGH)
        else:
            eye = jnp.eye(gain.shape[0], dtype=gain.dtype)
            through = jnp.dot(eye + first_gain, gain, precision=lax.Precision.HIGHEST)
            columns = lax.dynamic_slice_in_dim(through, first, per_device, 1)

            def part(rows, cut=None):
                base, src = own[:, rows], whole[:, rows]
                if cut is not None:
                    base, src = base[..., :cut], src[..., :cut]
                return base + jnp.einsum("kj,k...->j...", columns, src, precision=lax.Precision.HIGH)

            return (
                part(slice(0, f_in)),
                part(f_in + outs),
                part(slice(f_in, f_in + outs)),
                part(f_in + outs + 1, outs),
            )
    return unpack(own, f_in, hid, outs)


def solution(mesh):
    placed = (
        P("dp", None),
        P("member", "dp"),
        P(None, None, "member", "dp"),
        P("member", None, "dp"),
        P("member", "dp"),
        P("member", None, "dp"),
        P("member", None),
    )
    return jax.shard_map(
        on_device,
        mesh=mesh,
        in_specs=placed,
        out_specs=(
            P("member", None, "dp"),
            P("member", "dp"),
            P("member", None, "dp"),
            P("member", None),
        ),
        check_vma=False,
    )
```

```python
import functools

import jax
import jax.numpy as jnp
from jax import lax
from jax.experimental import pallas as pl
from jax.sharding import PartitionSpec as P

UPDATES = 2


ridge_level = 0.5


def solve_gain(gram, cross):
    eye = jnp.eye(gram.shape[0], dtype=gram.dtype)
    factor = jnp.linalg.cholesky(gram + ridge_level * eye)
    middle = lax.linalg.triangular_solve(factor, cross, left_side=True, lower=True)
    return lax.linalg.triangular_solve(factor, middle, left_side=True, lower=True, transpose_a=True)


def _eliminate(s_ref, o_ref, *, scale, ridge):
    a = s_ref[0] * scale
    b = s_ref[1] * scale
    n = a.shape[0]
    rows = lax.broadcasted_iota(jnp.int32, a.shape, 0)
    cols = lax.broadcasted_iota(jnp.int32, a.shape, 1)
    a = jnp.where(rows == cols, a + ridge, a)
    for k in range(n):
        pivot = a[k : k + 1, k : k + 1]
        ra = a[k : k + 1, :] / pivot
        rb = b[k : k + 1, :] / pivot
        col = a[:, k : k + 1]
        a = jnp.where(rows == k, ra, a - col * ra)
        b = jnp.where(rows == k, rb, b - col * rb)
    o_ref[...] = b

def solve_spd(sums, scale, ridge):
    kernel = functools.partial(_eliminate, scale=scale, ridge=ridge)
    return pl.pallas_call(kernel, out_shape=jax.ShapeDtypeStruct(sums.shape[1:], sums.dtype))(sums)

def pack(w_in, b_in, w_out, b_out):
    n, hid = w_in.shape[0], w_in.shape[2]
    pad = jnp.zeros((n, hid - b_out.shape[1]), b_out.dtype)
    return jnp.concatenate(
        [w_in, w_out, b_in[:, None, :], jnp.concatenate([b_out, pad], axis=1)[:, None, :]], axis=1
    )


def unpack(flat, f_in, hid, outs):
    return (
        flat[:, :f_in, :],
        flat[:, f_in + outs, :],
        flat[:, f_in : f_in + outs, :],
        flat[:, f_in + outs + 1, :outs],
    )


def gather_sum(x, axis):
    n = lax.axis_size(axis)
    flat = x.reshape(-1, 128)
    tiles = jnp.broadcast_to(flat[None], (n,) + flat.shape)
    got = lax.all_to_all(tiles, axis, split_axis=0, concat_axis=0, tiled=True)
    return jnp.sum(got, axis=0).reshape(x.shape)


def combine(columns, stack):
    expand = (slice(None), slice(None)) + (None,) * (stack.ndim - 1)
    return jnp.sum(columns[expand] * stack[:, None], axis=0)


def swap_pair(x):
    n = lax.axis_size("dp")
    return lax.ppermute(x, "dp", [(i, i ^ 1) for i in range(n)])


def predict(inputs_pair, own_flat, f_in, hid, outs, parity):
    n_dp = lax.axis_size("dp")
    rows = f_in + outs + 1
    rounded = own_flat[:, :rows, :].astype(jnp.bfloat16)
    n = rounded.shape[0]
    tiles = jnp.broadcast_to(rounded[None], (n_dp // n,) + rounded.shape).reshape((n_dp,) + rounded.shape[1:])
    got = lax.all_to_all(tiles, "dp", split_axis=0, concat_axis=0, tiled=True)
    w_in = got[:, :f_in, :]
    w_out = got[:, f_in : f_in + outs, :]
    b_in = got[:, f_in + outs, :]
    b_out = jnp.where(parity == 0, own_flat[0, rows, :outs], own_flat[1, rows, :outs])
    pre = jnp.einsum("sf,dfh->sdh", inputs_pair, w_in, preferred_element_type=jnp.float32)
    pre = pre + b_in.astype(jnp.float32)[None]
    hidden = jnp.tanh(pre).astype(jnp.bfloat16)
    pred = jnp.einsum("doh,sdh->os", w_out, hidden, preferred_element_type=jnp.float32)
    return pred + b_out[:, None]


def collect(pred, n_samples, parity):
    n_m = lax.axis_size("member")
    outs = pred.shape[0]
    blocks = pred.reshape(n_m, outs // n_m, pred.shape[1])
    got = lax.all_to_all(blocks, "member", split_axis=0, concat_axis=0, tiled=True)
    mine = got[:, :, :n_samples]
    other = swap_pair(got[:, :, n_samples:])
    even = jnp.where(parity == 0, mine, other)
    odd = jnp.where(parity == 0, other, mine)
    return jnp.stack([even, odd], axis=1).reshape(2 * n_m, outs // n_m, n_samples)


def on_device(inputs, observed, noise, w_in, b_in, w_out, b_out):
    per_device = w_in.shape[0]
    f_in, hid = w_in.shape[1], w_in.shape[2]
    outs = w_out.shape[1]
    n_samples = inputs.shape[0]
    count = observed.shape[0] * lax.axis_size("member") * observed.shape[1] * lax.axis_size("dp")
    first = lax.axis_index("member") * per_device
    parity = lax.axis_index("dp") % 2
    inputs_pair = jnp.concatenate([inputs, swap_pair(inputs)], axis=0)
    own = pack(w_in, b_in, w_out, b_out)
    whole = lax.all_gather(own, "member", axis=0, tiled=True)
    assert UPDATES == 2
    for update in range(UPDATES):
        predicted = predict(inputs_pair, own, f_in, hid, outs, parity)
        collected = collect(predicted, n_samples, parity)
        mean_pred = jnp.mean(collected, axis=0)
        anomaly = (collected - mean_pred[None]).reshape(collected.shape[0], -1)
        misfit = (observed[None] + noise[update].astype(jnp.float32) - collected).reshape(
            collected.shape[0], -1
        )
        gram_part = lax.dot_general(
            anomaly, anomaly, (((1,), (1,)), ((), ())), precision=lax.Precision.HIGHEST
        )
        cross_part = lax.dot_general(
            anomaly, misfit, (((1,), (1,)), ((), ())), precision=lax.Precision.HIGHEST
        )
        sums = gather_sum(gather_sum(jnp.stack([gram_part, cross_part]), "member"), "dp")
        if update == 0:
            sums = sums + whole[0, 0, 0] * 0
        gain = solve_spd(sums, 1.0 / count, ridge_level)
        if update == 0:
            first_gain = gain
            columns = lax.dynamic_slice_in_dim(gain, first, per_device, 1)
            own = own + combine(columns, whole)
        else:
            eye = jnp.eye(gain.shape[0], dtype=gain.dtype)
            through = jnp.dot(eye + first_gain, gain, precision=lax.Precision.HIGHEST)
            columns = lax.dynamic_slice_in_dim(through, first, per_device, 1)

            def part(rows, cut=None):
                base, src = own[:, rows], whole[:, rows]
                if cut is not None:
                    base, src = base[..., :cut], src[..., :cut]
                return base + combine(columns, src)

            return (
                part(slice(0, f_in)),
                part(f_in + outs),
                part(slice(f_in, f_in + outs)),
                part(f_in + outs + 1, outs),
            )
    return unpack(own, f_in, hid, outs)


def solution(mesh):
    placed = (
        P("dp", None),
        P("member", "dp"),
        P(None, None, "member", "dp"),
        P("member", None, "dp"),
        P("member", "dp"),
        P("member", None, "dp"),
        P("member", None),
    )
    return jax.shard_map(
        on_device,
        mesh=mesh,
        in_specs=placed,
        out_specs=(
            P("member", None, "dp"),
            P("member", "dp"),
            P("member", None, "dp"),
            P("member", None),
        ),
        check_vma=False,
    )
```

```python
import functools

import jax
import jax.numpy as jnp
from jax import lax
from jax.experimental import pallas as pl
from jax.sharding import PartitionSpec as P

UPDATES = 2


ridge_level = 0.5


def solve_gain(gram, cross):
    eye = jnp.eye(gram.shape[0], dtype=gram.dtype)
    factor = jnp.linalg.cholesky(gram + ridge_level * eye)
    middle = lax.linalg.triangular_solve(factor, cross, left_side=True, lower=True)
    return lax.linalg.triangular_solve(factor, middle, left_side=True, lower=True, transpose_a=True)


def _eliminate(s_ref, o_ref, *, scale, ridge):
    a = s_ref[0] * scale
    b = s_ref[1] * scale
    n = a.shape[0]
    rows = lax.broadcasted_iota(jnp.int32, a.shape, 0)
    cols = lax.broadcasted_iota(jnp.int32, a.shape, 1)
    a = jnp.where(rows == cols, a + ridge, a)
    for k in range(n):
        pivot = a[k : k + 1, k : k + 1]
        ra = a[k : k + 1, :] / pivot
        rb = b[k : k + 1, :] / pivot
        col = a[:, k : k + 1]
        a = jnp.where(rows == k, ra, a - col * ra)
        b = jnp.where(rows == k, rb, b - col * rb)
    o_ref[...] = b

def solve_spd(sums, scale, ridge):
    kernel = functools.partial(_eliminate, scale=scale, ridge=ridge)
    return pl.pallas_call(kernel, out_shape=jax.ShapeDtypeStruct(sums.shape[1:], sums.dtype))(sums)

def pack(w_in, b_in, w_out, b_out):
    n, hid = w_in.shape[0], w_in.shape[2]
    pad = jnp.zeros((n, hid - b_out.shape[1]), b_out.dtype)
    return jnp.concatenate(
        [w_in, w_out, b_in[:, None, :], jnp.concatenate([b_out, pad], axis=1)[:, None, :]], axis=1
    )


def unpack(flat, f_in, hid, outs):
    return (
        flat[:, :f_in, :],
        flat[:, f_in + outs, :],
        flat[:, f_in : f_in + outs, :],
        flat[:, f_in + outs + 1, :outs],
    )


def gather_sum(x, axis):
    n = lax.axis_size(axis)
    flat = x.reshape(-1, 128)
    tiles = jnp.broadcast_to(flat[None], (n,) + flat.shape)
    got = lax.all_to_all(tiles, axis, split_axis=0, concat_axis=0, tiled=True)
    return jnp.sum(got, axis=0).reshape(x.shape)


def swap_pair(x):
    n = lax.axis_size("dp")
    return lax.ppermute(x, "dp", [(i, i ^ 1) for i in range(n)])


def predict(inputs_pair, own_flat, f_in, hid, outs, parity):
    n_dp = lax.axis_size("dp")
    rows = f_in + outs + 1
    rounded = own_flat[:, :rows, :].astype(jnp.bfloat16)
    n = rounded.shape[0]
    tiles = jnp.broadcast_to(rounded[None], (n_dp // n,) + rounded.shape).reshape((n_dp,) + rounded.shape[1:])
    got = lax.all_to_all(tiles, "dp", split_axis=0, concat_axis=0, tiled=True)
    w_in = got[:, :f_in, :]
    w_out = got[:, f_in : f_in + outs, :]
    b_in = got[:, f_in + outs, :]
    b_out = jnp.where(parity == 0, own_flat[0, rows, :outs], own_flat[1, rows, :outs])
    pre = jnp.einsum("sf,dfh->sdh", inputs_pair, w_in, preferred_element_type=jnp.float32)
    pre = pre + b_in.astype(jnp.float32)[None]
    hidden = jnp.tanh(pre).astype(jnp.bfloat16)
    pred = jnp.einsum("doh,sdh->os", w_out, hidden, preferred_element_type=jnp.float32)
    return pred + b_out[:, None]


def collect(pred, n_samples, parity):
    n_m = lax.axis_size("member")
    outs = pred.shape[0]
    blocks = pred.reshape(n_m, outs // n_m, pred.shape[1])
    got = lax.all_to_all(blocks, "member", split_axis=0, concat_axis=0, tiled=True)
    mine = got[:, :, :n_samples]
    other = swap_pair(got[:, :, n_samples:])
    even = jnp.where(parity == 0, mine, other)
    odd = jnp.where(parity == 0, other, mine)
    return jnp.stack([even, odd], axis=1).reshape(2 * n_m, outs // n_m, n_samples)


def on_device(inputs, observed, noise, w_in, b_in, w_out, b_out):
    per_device = w_in.shape[0]
    f_in, hid = w_in.shape[1], w_in.shape[2]
    outs = w_out.shape[1]
    n_samples = inputs.shape[0]
    count = observed.shape[0] * lax.axis_size("member") * observed.shape[1] * lax.axis_size("dp")
    first = lax.axis_index("member") * per_device
    parity = lax.axis_index("dp") % 2
    inputs_pair = jnp.concatenate([inputs, swap_pair(inputs)], axis=0)
    own = pack(w_in, b_in, w_out, b_out)
    whole = lax.all_gather(own, "member", axis=0, tiled=True)
    assert UPDATES == 2
    for update in range(UPDATES):
        predicted = predict(inputs_pair, own, f_in, hid, outs, parity)
        collected = collect(predicted, n_samples, parity)
        mean_pred = jnp.mean(collected, axis=0)
        anomaly = (collected - mean_pred[None]).reshape(collected.shape[0], -1)
        misfit = (observed[None] + noise[update].astype(jnp.float32) - collected).reshape(
            collected.shape[0], -1
        )
        gram_part = lax.dot_general(
            anomaly, anomaly, (((1,), (1,)), ((), ())), precision=lax.Precision.HIGHEST
        )
        cross_part = lax.dot_general(
            anomaly, misfit, (((1,), (1,)), ((), ())), precision=lax.Precision.HIGHEST
        )
        sums = gather_sum(gather_sum(jnp.stack([gram_part, cross_part]), "dp"), "member")
        if update == 0:
            sums = sums + whole[0, 0, 0] * 0
        gain = solve_spd(sums, 1.0 / count, ridge_level)
        if update == 0:
            first_gain = gain
            columns = lax.dynamic_slice_in_dim(gain, first, per_device, 1)
            own = own + jnp.einsum("kj,kab->jab", columns, whole, precision=lax.Precision.HIGH)
        else:
            eye = jnp.eye(gain.shape[0], dtype=gain.dtype)
            through = jnp.dot(eye + first_gain, gain, precision=lax.Precision.HIGHEST)
            columns = lax.dynamic_slice_in_dim(through, first, per_device, 1)

            def part(rows, cut=None):
                base, src = own[:, rows], whole[:, rows]
                if cut is not None:
                    base, src = base[..., :cut], src[..., :cut]
                return base + jnp.einsum("kj,k...->j...", columns, src, precision=lax.Precision.HIGH)

            return (
                part(slice(0, f_in)),
                part(f_in + outs),
                part(slice(f_in, f_in + outs)),
                part(f_in + outs + 1, outs),
            )
    return unpack(own, f_in, hid, outs)


def solution(mesh):
    placed = (
        P("dp", None),
        P("member", "dp"),
        P(None, None, "member", "dp"),
        P("member", None, "dp"),
        P("member", "dp"),
        P("member", None, "dp"),
        P("member", None),
    )
    return jax.shard_map(
        on_device,
        mesh=mesh,
        in_specs=placed,
        out_specs=(
            P("member", None, "dp"),
            P("member", "dp"),
            P("member", None, "dp"),
            P("member", None),
        ),
        check_vma=False,
    )
```

```python
import functools

import jax
import jax.numpy as jnp
from jax import lax
from jax.experimental import pallas as pl
from jax.experimental.pallas import tpu as pltpu
from jax.sharding import PartitionSpec as P

UPDATES = 2


ridge_level = 0.5


def solve_gain(gram, cross):
    eye = jnp.eye(gram.shape[0], dtype=gram.dtype)
    factor = jnp.linalg.cholesky(gram + ridge_level * eye)
    middle = lax.linalg.triangular_solve(factor, cross, left_side=True, lower=True)
    return lax.linalg.triangular_solve(factor, middle, left_side=True, lower=True, transpose_a=True)


def _eliminate(s_ref, *rest, scale, ridge):
    o_ref = rest[-1]
    a = s_ref[0] * scale
    b = s_ref[1] * scale
    n = a.shape[0]
    rows = lax.broadcasted_iota(jnp.int32, a.shape, 0)
    cols = lax.broadcasted_iota(jnp.int32, a.shape, 1)
    a = jnp.where(rows == cols, a + ridge, a)
    for k in range(n):
        pivot = a[k : k + 1, k : k + 1]
        ra = a[k : k + 1, :] / pivot
        rb = b[k : k + 1, :] / pivot
        col = a[:, k : k + 1]
        a = jnp.where(rows == k, ra, a - col * ra)
        b = jnp.where(rows == k, rb, b - col * rb)
    o_ref[...] = b


def solve_spd(sums, scale, ridge, after=()):
    kernel = functools.partial(_eliminate, scale=scale, ridge=ridge)
    specs = [pl.BlockSpec(memory_space=pltpu.VMEM)] + [pl.BlockSpec(memory_space=pl.ANY) for _ in after]
    return pl.pallas_call(
        kernel,
        out_shape=jax.ShapeDtypeStruct(sums.shape[1:], sums.dtype),
        in_specs=specs,
        out_specs=pl.BlockSpec(memory_space=pltpu.VMEM),
    )(sums, *after)


def pack(w_in, b_in, w_out, b_out):
    n, hid = w_in.shape[0], w_in.shape[2]
    pad = jnp.zeros((n, hid - b_out.shape[1]), b_out.dtype)
    return jnp.concatenate(
        [w_in, w_out, b_in[:, None, :], jnp.concatenate([b_out, pad], axis=1)[:, None, :]], axis=1
    )


def unpack(flat, f_in, hid, outs):
    return (
        flat[:, :f_in, :],
        flat[:, f_in + outs, :],
        flat[:, f_in : f_in + outs, :],
        flat[:, f_in + outs + 1, :outs],
    )


def gather_sum(x, axis):
    n = lax.axis_size(axis)
    flat = x.reshape(-1, 128)
    tiles = jnp.broadcast_to(flat[None], (n,) + flat.shape)
    got = lax.all_to_all(tiles, axis, split_axis=0, concat_axis=0, tiled=True)
    return jnp.sum(got, axis=0).reshape(x.shape)


def swap_pair(x):
    n = lax.axis_size("dp")
    return lax.ppermute(x, "dp", [(i, i ^ 1) for i in range(n)])


def predict(inputs_pair, own_flat, f_in, hid, outs, parity):
    n_dp = lax.axis_size("dp")
    rows = f_in + outs + 1
    rounded = own_flat[:, :rows, :].astype(jnp.bfloat16)
    n = rounded.shape[0]
    tiles = jnp.broadcast_to(rounded[None], (n_dp // n,) + rounded.shape).reshape((n_dp,) + rounded.shape[1:])
    got = lax.all_to_all(tiles, "dp", split_axis=0, concat_axis=0, tiled=True)
    w_in = got[:, :f_in, :]
    w_out = got[:, f_in : f_in + outs, :]
    b_in = got[:, f_in + outs, :]
    b_out = jnp.where(parity == 0, own_flat[0, rows, :outs], own_flat[1, rows, :outs])
    pre = jnp.einsum("sf,dfh->sdh", inputs_pair, w_in, preferred_element_type=jnp.float32)
    pre = pre + b_in.astype(jnp.float32)[None]
    hidden = jnp.tanh(pre).astype(jnp.bfloat16)
    pred = jnp.einsum("doh,sdh->os", w_out, hidden, preferred_element_type=jnp.float32)
    return pred + b_out[:, None]


def collect(pred, n_samples, parity):
    n_m = lax.axis_size("member")
    outs = pred.shape[0]
    blocks = pred.reshape(n_m, outs // n_m, pred.shape[1])
    got = lax.all_to_all(blocks, "member", split_axis=0, concat_axis=0, tiled=True)
    mine = got[:, :, :n_samples]
    other = swap_pair(got[:, :, n_samples:])
    even = jnp.where(parity == 0, mine, other)
    odd = jnp.where(parity == 0, other, mine)
    return jnp.stack([even, odd], axis=1).reshape(2 * n_m, outs // n_m, n_samples)


def on_device(inputs, observed, noise, w_in, b_in, w_out, b_out):
    per_device = w_in.shape[0]
    f_in, hid = w_in.shape[1], w_in.shape[2]
    outs = w_out.shape[1]
    n_samples = inputs.shape[0]
    count = observed.shape[0] * lax.axis_size("member") * observed.shape[1] * lax.axis_size("dp")
    first = lax.axis_index("member") * per_device
    parity = lax.axis_index("dp") % 2
    inputs_pair = jnp.concatenate([inputs, swap_pair(inputs)], axis=0)
    own = pack(w_in, b_in, w_out, b_out)
    whole = lax.all_gather(own, "member", axis=0, tiled=True)
    assert UPDATES == 2
    for update in range(UPDATES):
        predicted = predict(inputs_pair, own, f_in, hid, outs, parity)
        collected = collect(predicted, n_samples, parity)
        mean_pred = jnp.mean(collected, axis=0)
        anomaly = (collected - mean_pred[None]).reshape(collected.shape[0], -1)
        misfit = (observed[None] + noise[update].astype(jnp.float32) - collected).reshape(
            collected.shape[0], -1
        )
        gram_part = lax.dot_general(
            anomaly, anomaly, (((1,), (1,)), ((), ())), precision=lax.Precision.HIGHEST
        )
        cross_part = lax.dot_general(
            anomaly, misfit, (((1,), (1,)), ((), ())), precision=lax.Precision.HIGHEST
        )
        sums = gather_sum(gather_sum(jnp.stack([gram_part, cross_part]), "dp"), "member")
        gain = solve_spd(sums, 1.0 / count, ridge_level, (whole,) if update == 0 else ())
        if update == 0:
            first_gain = gain
            columns = lax.dynamic_slice_in_dim(gain, first, per_device, 1)
            own = own + jnp.einsum("kj,kab->jab", columns, whole, precision=lax.Precision.HIGH)
        else:
            eye = jnp.eye(gain.shape[0], dtype=gain.dtype)
            through = jnp.dot(eye + first_gain, gain, precision=lax.Precision.HIGHEST)
            columns = lax.dynamic_slice_in_dim(through, first, per_device, 1)

            def part(rows, cut=None):
                base, src = own[:, rows], whole[:, rows]
                if cut is not None:
                    base, src = base[..., :cut], src[..., :cut]
                return base + jnp.einsum("kj,k...->j...", columns, src, precision=lax.Precision.HIGH)

            return (
                part(slice(0, f_in)),
                part(f_in + outs),
                part(slice(f_in, f_in + outs)),
                part(f_in + outs + 1, outs),
            )
    return unpack(own, f_in, hid, outs)


def solution(mesh):
    placed = (
        P("dp", None),
        P("member", "dp"),
        P(None, None, "member", "dp"),
        P("member", None, "dp"),
        P("member", "dp"),
        P("member", None, "dp"),
        P("member", None),
    )
    return jax.shard_map(
        on_device,
        mesh=mesh,
        in_specs=placed,
        out_specs=(
            P("member", None, "dp"),
            P("member", "dp"),
            P("member", None, "dp"),
            P("member", None),
        ),
        check_vma=False,
    )
```

```python
import functools

import jax
import jax.numpy as jnp
from jax import lax
from jax.experimental import pallas as pl
from jax.experimental.pallas import tpu as pltpu
from jax.sharding import PartitionSpec as P

UPDATES = 2


ridge_level = 0.5


def solve_gain(gram, cross):
    eye = jnp.eye(gram.shape[0], dtype=gram.dtype)
    factor = jnp.linalg.cholesky(gram + ridge_level * eye)
    middle = lax.linalg.triangular_solve(factor, cross, left_side=True, lower=True)
    return lax.linalg.triangular_solve(factor, middle, left_side=True, lower=True, transpose_a=True)


def _eliminate(s_ref, *rest, scale, ridge):
    o_ref = rest[-1]
    a = s_ref[0] * scale
    b = s_ref[1] * scale
    n = a.shape[0]
    rows = lax.broadcasted_iota(jnp.int32, a.shape, 0)
    cols = lax.broadcasted_iota(jnp.int32, a.shape, 1)
    a = jnp.where(rows == cols, a + ridge, a)
    for k in range(n):
        inverse = 1.0 / a[k : k + 1, k : k + 1]
        ra = a[k : k + 1, :] * inverse
        rb = b[k : k + 1, :] * inverse
        col = a[:, k : k + 1]
        a = jnp.where(rows == k, ra, a - col * ra)
        b = jnp.where(rows == k, rb, b - col * rb)
    o_ref[...] = b


def solve_spd(sums, scale, ridge, after=()):
    kernel = functools.partial(_eliminate, scale=scale, ridge=ridge)
    specs = [pl.BlockSpec(memory_space=pltpu.VMEM)] + [pl.BlockSpec(memory_space=pl.ANY) for _ in after]
    return pl.pallas_call(
        kernel,
        out_shape=jax.ShapeDtypeStruct(sums.shape[1:], sums.dtype),
        in_specs=specs,
        out_specs=pl.BlockSpec(memory_space=pltpu.VMEM),
    )(sums, *after)


def pack(w_in, b_in, w_out, b_out):
    n, hid = w_in.shape[0], w_in.shape[2]
    pad = jnp.zeros((n, hid - b_out.shape[1]), b_out.dtype)
    return jnp.concatenate(
        [w_in, w_out, b_in[:, None, :], jnp.concatenate([b_out, pad], axis=1)[:, None, :]], axis=1
    )


def unpack(flat, f_in, hid, outs):
    return (
        flat[:, :f_in, :],
        flat[:, f_in + outs, :],
        flat[:, f_in : f_in + outs, :],
        flat[:, f_in + outs + 1, :outs],
    )


def gather_sum(x, axis):
    n = lax.axis_size(axis)
    flat = x.reshape(-1, 128)
    tiles = jnp.broadcast_to(flat[None], (n,) + flat.shape)
    got = lax.all_to_all(tiles, axis, split_axis=0, concat_axis=0, tiled=True)
    return jnp.sum(got, axis=0).reshape(x.shape)


def swap_pair(x):
    n = lax.axis_size("dp")
    return lax.ppermute(x, "dp", [(i, i ^ 1) for i in range(n)])


def predict(inputs_pair, own_flat, f_in, hid, outs, parity):
    n_dp = lax.axis_size("dp")
    rows = f_in + outs + 1
    rounded = own_flat[:, :rows, :].astype(jnp.bfloat16)
    n = rounded.shape[0]
    tiles = jnp.broadcast_to(rounded[None], (n_dp // n,) + rounded.shape).reshape((n_dp,) + rounded.shape[1:])
    got = lax.all_to_all(tiles, "dp", split_axis=0, concat_axis=0, tiled=True)
    w_in = got[:, :f_in, :]
    w_out = got[:, f_in : f_in + outs, :]
    b_in = got[:, f_in + outs, :]
    b_out = jnp.where(parity == 0, own_flat[0, rows, :outs], own_flat[1, rows, :outs])
    pre = jnp.einsum("sf,dfh->sdh", inputs_pair, w_in, preferred_element_type=jnp.float32)
    pre = pre + b_in.astype(jnp.float32)[None]
    hidden = jnp.tanh(pre).astype(jnp.bfloat16)
    pred = jnp.einsum("doh,sdh->os", w_out, hidden, preferred_element_type=jnp.float32)
    return pred + b_out[:, None]


def collect(pred, n_samples, parity):
    n_m = lax.axis_size("member")
    outs = pred.shape[0]
    blocks = pred.reshape(n_m, outs // n_m, pred.shape[1])
    got = lax.all_to_all(blocks, "member", split_axis=0, concat_axis=0, tiled=True)
    mine = got[:, :, :n_samples]
    other = swap_pair(got[:, :, n_samples:])
    even = jnp.where(parity == 0, mine, other)
    odd = jnp.where(parity == 0, other, mine)
    return jnp.stack([even, odd], axis=1).reshape(2 * n_m, outs // n_m, n_samples)


def on_device(inputs, observed, noise, w_in, b_in, w_out, b_out):
    per_device = w_in.shape[0]
    f_in, hid = w_in.shape[1], w_in.shape[2]
    outs = w_out.shape[1]
    n_samples = inputs.shape[0]
    count = observed.shape[0] * lax.axis_size("member") * observed.shape[1] * lax.axis_size("dp")
    first = lax.axis_index("member") * per_device
    parity = lax.axis_index("dp") % 2
    inputs_pair = jnp.concatenate([inputs, swap_pair(inputs)], axis=0)
    own = pack(w_in, b_in, w_out, b_out)
    whole = lax.all_gather(own, "member", axis=0, tiled=True)
    assert UPDATES == 2
    for update in range(UPDATES):
        predicted = predict(inputs_pair, own, f_in, hid, outs, parity)
        collected = collect(predicted, n_samples, parity)
        mean_pred = jnp.mean(collected, axis=0)
        anomaly = (collected - mean_pred[None]).reshape(collected.shape[0], -1)
        misfit = (observed[None] + noise[update].astype(jnp.float32) - collected).reshape(
            collected.shape[0], -1
        )
        gram_part = lax.dot_general(
            anomaly, anomaly, (((1,), (1,)), ((), ())), precision=lax.Precision.HIGHEST
        )
        cross_part = lax.dot_general(
            anomaly, misfit, (((1,), (1,)), ((), ())), precision=lax.Precision.HIGHEST
        )
        sums = gather_sum(gather_sum(jnp.stack([gram_part, cross_part]), "dp"), "member")
        gain = solve_spd(sums, 1.0 / count, ridge_level, (whole,) if update == 0 else ())
        if update == 0:
            first_gain = gain
            columns = lax.dynamic_slice_in_dim(gain, first, per_device, 1)
            own = own + jnp.einsum("kj,kab->jab", columns, whole, precision=lax.Precision.HIGH)
        else:
            eye = jnp.eye(gain.shape[0], dtype=gain.dtype)
            through = jnp.dot(eye + first_gain, gain, precision=lax.Precision.HIGHEST)
            columns = lax.dynamic_slice_in_dim(through, first, per_device, 1)

            def part(rows, cut=None):
                base, src = own[:, rows], whole[:, rows]
                if cut is not None:
                    base, src = base[..., :cut], src[..., :cut]
                return base + jnp.einsum("kj,k...->j...", columns, src, precision=lax.Precision.HIGH)

            return (
                part(slice(0, f_in)),
                part(f_in + outs),
                part(slice(f_in, f_in + outs)),
                part(f_in + outs + 1, outs),
            )
    return unpack(own, f_in, hid, outs)


def solution(mesh):
    placed = (
        P("dp", None),
        P("member", "dp"),
        P(None, None, "member", "dp"),
        P("member", None, "dp"),
        P("member", "dp"),
        P("member", None, "dp"),
        P("member", None),
    )
    return jax.shard_map(
        on_device,
        mesh=mesh,
        in_specs=placed,
        out_specs=(
            P("member", None, "dp"),
            P("member", "dp"),
            P("member", None, "dp"),
            P("member", None),
        ),
        check_vma=False,
    )
```

```python
import functools

import jax
import jax.numpy as jnp
from jax import lax
from jax.experimental import pallas as pl
from jax.experimental.pallas import tpu as pltpu
from jax.sharding import PartitionSpec as P

UPDATES = 2


ridge_level = 0.5


def solve_gain(gram, cross):
    eye = jnp.eye(gram.shape[0], dtype=gram.dtype)
    factor = jnp.linalg.cholesky(gram + ridge_level * eye)
    middle = lax.linalg.triangular_solve(factor, cross, left_side=True, lower=True)
    return lax.linalg.triangular_solve(factor, middle, left_side=True, lower=True, transpose_a=True)


def _eliminate(s_ref, *rest, scale, ridge):
    o_ref = rest[-1]
    n = o_ref.shape[0]
    total = jnp.sum(s_ref[...], axis=0)
    a = total[:, :n] * scale
    b = total[:, n : 2 * n] * scale
    rows = lax.broadcasted_iota(jnp.int32, a.shape, 0)
    cols = lax.broadcasted_iota(jnp.int32, a.shape, 1)
    a = jnp.where(rows == cols, a + ridge, a)
    for k in range(n):
        pivot = a[k : k + 1, k : k + 1]
        ra = a[k : k + 1, :] / pivot
        rb = b[k : k + 1, :] / pivot
        col = a[:, k : k + 1]
        a = jnp.where(rows == k, ra, a - col * ra)
        b = jnp.where(rows == k, rb, b - col * rb)
    o_ref[...] = b


def solve_spd(sums, scale, ridge, after=()):
    kernel = functools.partial(_eliminate, scale=scale, ridge=ridge)
    specs = [pl.BlockSpec(memory_space=pltpu.VMEM)] + [pl.BlockSpec(memory_space=pl.ANY) for _ in after]
    return pl.pallas_call(
        kernel,
        out_shape=jax.ShapeDtypeStruct((sums.shape[1], sums.shape[1]), sums.dtype),
        in_specs=specs,
        out_specs=pl.BlockSpec(memory_space=pltpu.VMEM),
    )(sums, *after)


def pack(w_in, b_in, w_out, b_out):
    n, hid = w_in.shape[0], w_in.shape[2]
    pad = jnp.zeros((n, hid - b_out.shape[1]), b_out.dtype)
    return jnp.concatenate(
        [w_in, w_out, b_in[:, None, :], jnp.concatenate([b_out, pad], axis=1)[:, None, :]], axis=1
    )


def unpack(flat, f_in, hid, outs):
    return (
        flat[:, :f_in, :],
        flat[:, f_in + outs, :],
        flat[:, f_in : f_in + outs, :],
        flat[:, f_in + outs + 1, :outs],
    )


def gather_sum(x, axis):
    n = lax.axis_size(axis)
    flat = x.reshape(-1, 128)
    tiles = jnp.broadcast_to(flat[None], (n,) + flat.shape)
    got = lax.all_to_all(tiles, axis, split_axis=0, concat_axis=0, tiled=True)
    return jnp.sum(got, axis=0).reshape(x.shape)


def gather_stack(x, axis):
    n = lax.axis_size(axis)
    tiles = jnp.broadcast_to(x[None], (n,) + x.shape)
    return lax.all_to_all(tiles, axis, split_axis=0, concat_axis=0, tiled=True)


def swap_pair(x):
    n = lax.axis_size("dp")
    return lax.ppermute(x, "dp", [(i, i ^ 1) for i in range(n)])


def predict(inputs_pair, own_flat, f_in, hid, outs, parity):
    n_dp = lax.axis_size("dp")
    rows = f_in + outs + 1
    rounded = own_flat[:, :rows, :].astype(jnp.bfloat16)
    n = rounded.shape[0]
    tiles = jnp.broadcast_to(rounded[None], (n_dp // n,) + rounded.shape).reshape((n_dp,) + rounded.shape[1:])
    got = lax.all_to_all(tiles, "dp", split_axis=0, concat_axis=0, tiled=True)
    w_in = got[:, :f_in, :]
    w_out = got[:, f_in : f_in + outs, :]
    b_in = got[:, f_in + outs, :]
    b_out = jnp.where(parity == 0, own_flat[0, rows, :outs], own_flat[1, rows, :outs])
    pre = jnp.einsum("sf,dfh->sdh", inputs_pair, w_in, preferred_element_type=jnp.float32)
    pre = pre + b_in.astype(jnp.float32)[None]
    hidden = jnp.tanh(pre).astype(jnp.bfloat16)
    pred = jnp.einsum("doh,sdh->os", w_out, hidden, preferred_element_type=jnp.float32)
    return pred + b_out[:, None]


def collect(pred, n_samples, parity):
    n_m = lax.axis_size("member")
    outs = pred.shape[0]
    blocks = pred.reshape(n_m, outs // n_m, pred.shape[1])
    got = lax.all_to_all(blocks, "member", split_axis=0, concat_axis=0, tiled=True)
    mine = got[:, :, :n_samples]
    other = swap_pair(got[:, :, n_samples:])
    even = jnp.where(parity == 0, mine, other)
    odd = jnp.where(parity == 0, other, mine)
    return jnp.stack([even, odd], axis=1).reshape(2 * n_m, outs // n_m, n_samples)


def on_device(inputs, observed, noise, w_in, b_in, w_out, b_out):
    per_device = w_in.shape[0]
    f_in, hid = w_in.shape[1], w_in.shape[2]
    outs = w_out.shape[1]
    n_samples = inputs.shape[0]
    count = observed.shape[0] * lax.axis_size("member") * observed.shape[1] * lax.axis_size("dp")
    first = lax.axis_index("member") * per_device
    parity = lax.axis_index("dp") % 2
    inputs_pair = jnp.concatenate([inputs, swap_pair(inputs)], axis=0)
    own = pack(w_in, b_in, w_out, b_out)
    whole = lax.all_gather(own, "member", axis=0, tiled=True)
    assert UPDATES == 2
    for update in range(UPDATES):
        predicted = predict(inputs_pair, own, f_in, hid, outs, parity)
        collected = collect(predicted, n_samples, parity)
        mean_pred = jnp.mean(collected, axis=0)
        anomaly = (collected - mean_pred[None]).reshape(collected.shape[0], -1)
        misfit = (observed[None] + noise[update].astype(jnp.float32) - collected).reshape(
            collected.shape[0], -1
        )
        gram_part = lax.dot_general(
            anomaly, anomaly, (((1,), (1,)), ((), ())), precision=lax.Precision.HIGHEST
        )
        cross_part = lax.dot_general(
            anomaly, misfit, (((1,), (1,)), ((), ())), precision=lax.Precision.HIGHEST
        )
        pad = jnp.zeros((gram_part.shape[0], 128 - 2 * gram_part.shape[1]), gram_part.dtype)
        payload = jnp.concatenate([gram_part, cross_part, pad], axis=1)
        sums = gather_stack(gather_sum(payload, "dp"), "member")
        gain = solve_spd(sums, 1.0 / count, ridge_level, (whole,) if update == 0 else ())
        if update == 0:
            first_gain = gain
            columns = lax.dynamic_slice_in_dim(gain, first, per_device, 1)
            own = own + jnp.einsum("kj,kab->jab", columns, whole, precision=lax.Precision.HIGH)
        else:
            eye = jnp.eye(gain.shape[0], dtype=gain.dtype)
            through = jnp.dot(eye + first_gain, gain, precision=lax.Precision.HIGHEST)
            columns = lax.dynamic_slice_in_dim(through, first, per_device, 1)

            def part(rows, cut=None):
                base, src = own[:, rows], whole[:, rows]
                if cut is not None:
                    base, src = base[..., :cut], src[..., :cut]
                return base + jnp.einsum("kj,k...->j...", columns, src, precision=lax.Precision.HIGH)

            return (
                part(slice(0, f_in)),
                part(f_in + outs),
                part(slice(f_in, f_in + outs)),
                part(f_in + outs + 1, outs),
            )
    return unpack(own, f_in, hid, outs)


def solution(mesh):
    placed = (
        P("dp", None),
        P("member", "dp"),
        P(None, None, "member", "dp"),
        P("member", None, "dp"),
        P("member", "dp"),
        P("member", None, "dp"),
        P("member", None),
    )
    return jax.shard_map(
        on_device,
        mesh=mesh,
        in_specs=placed,
        out_specs=(
            P("member", None, "dp"),
            P("member", "dp"),
            P("member", None, "dp"),
            P("member", None),
        ),
        check_vma=False,
    )
```

```python
import functools

import jax
import jax.numpy as jnp
from jax import lax
from jax.experimental import pallas as pl
from jax.experimental.pallas import tpu as pltpu
from jax.sharding import PartitionSpec as P

UPDATES = 2


ridge_level = 0.5


def solve_gain(gram, cross):
    eye = jnp.eye(gram.shape[0], dtype=gram.dtype)
    factor = jnp.linalg.cholesky(gram + ridge_level * eye)
    middle = lax.linalg.triangular_solve(factor, cross, left_side=True, lower=True)
    return lax.linalg.triangular_solve(factor, middle, left_side=True, lower=True, transpose_a=True)


def _eliminate(s_ref, *rest, scale, ridge):
    o_ref = rest[-1]
    a = s_ref[0] * scale
    b = s_ref[1] * scale
    n = a.shape[0]
    rows = lax.broadcasted_iota(jnp.int32, a.shape, 0)
    cols = lax.broadcasted_iota(jnp.int32, a.shape, 1)
    a = jnp.where(rows == cols, a + ridge, a)
    for k in range(n):
        pivot = a[k : k + 1, k : k + 1]
        ra = a[k : k + 1, :] / pivot
        rb = b[k : k + 1, :] / pivot
        col = a[:, k : k + 1]
        a = jnp.where(rows == k, ra, a - col * ra)
        b = jnp.where(rows == k, rb, b - col * rb)
    o_ref[...] = b


def solve_spd(sums, scale, ridge, after=()):
    kernel = functools.partial(_eliminate, scale=scale, ridge=ridge)
    specs = [pl.BlockSpec(memory_space=pltpu.VMEM)] + [pl.BlockSpec(memory_space=pl.ANY) for _ in after]
    return pl.pallas_call(
        kernel,
        out_shape=jax.ShapeDtypeStruct(sums.shape[1:], sums.dtype),
        in_specs=specs,
        out_specs=pl.BlockSpec(memory_space=pltpu.VMEM),
    )(sums, *after)


def pack(w_in, b_in, w_out, b_out):
    n, hid = w_in.shape[0], w_in.shape[2]
    pad = jnp.zeros((n, hid - b_out.shape[1]), b_out.dtype)
    return jnp.concatenate(
        [w_in, w_out, b_in[:, None, :], jnp.concatenate([b_out, pad], axis=1)[:, None, :]], axis=1
    )


def unpack(flat, f_in, hid, outs):
    return (
        flat[:, :f_in, :],
        flat[:, f_in + outs, :],
        flat[:, f_in : f_in + outs, :],
        flat[:, f_in + outs + 1, :outs],
    )


def gather_sum(x, axis):
    n = lax.axis_size(axis)
    flat = x.reshape(-1, 128)
    tiles = jnp.broadcast_to(flat[None], (n,) + flat.shape)
    got = lax.all_to_all(tiles, axis, split_axis=0, concat_axis=0, tiled=True)
    return jnp.sum(got, axis=0).reshape(x.shape)


def swap_pair(x):
    n = lax.axis_size("dp")
    return lax.ppermute(x, "dp", [(i, i ^ 1) for i in range(n)])


def predict(inputs_pair, own_flat, f_in, hid, outs, parity):
    n_dp = lax.axis_size("dp")
    rows = f_in + outs + 1
    rounded = own_flat[:, :rows, :].astype(jnp.bfloat16)
    n = rounded.shape[0]
    tiles = jnp.broadcast_to(rounded[None], (n_dp // n,) + rounded.shape).reshape((n_dp,) + rounded.shape[1:])
    got = lax.all_to_all(tiles, "dp", split_axis=0, concat_axis=0, tiled=True)
    w_in = got[:, :f_in, :]
    w_out = got[:, f_in : f_in + outs, :]
    b_in = got[:, f_in + outs, :]
    b_out = jnp.where(parity == 0, own_flat[0, rows, :outs], own_flat[1, rows, :outs])
    pre = jnp.einsum("sf,dfh->sdh", inputs_pair, w_in, preferred_element_type=jnp.float32)
    pre = pre + b_in.astype(jnp.float32)[None]
    hidden = jnp.tanh(pre).astype(jnp.bfloat16)
    pred = jnp.einsum("doh,sdh->os", w_out, hidden, preferred_element_type=jnp.float32)
    return pred + b_out[:, None]


def collect(pred, n_samples, parity):
    n_m = lax.axis_size("member")
    outs = pred.shape[0]
    blocks = pred.reshape(n_m, outs // n_m, pred.shape[1])
    got = lax.all_to_all(blocks, "member", split_axis=0, concat_axis=0, tiled=True)
    mine = got[:, :, :n_samples]
    other = swap_pair(got[:, :, n_samples:])
    even = jnp.where(parity == 0, mine, other)
    odd = jnp.where(parity == 0, other, mine)
    return jnp.stack([even, odd], axis=1).reshape(2 * n_m, outs // n_m, n_samples)


def on_device(inputs, observed, noise, w_in, b_in, w_out, b_out):
    per_device = w_in.shape[0]
    f_in, hid = w_in.shape[1], w_in.shape[2]
    outs = w_out.shape[1]
    n_samples = inputs.shape[0]
    count = observed.shape[0] * lax.axis_size("member") * observed.shape[1] * lax.axis_size("dp")
    first = lax.axis_index("member") * per_device
    parity = lax.axis_index("dp") % 2
    inputs_pair = jnp.concatenate([inputs, swap_pair(inputs)], axis=0)
    own = pack(w_in, b_in, w_out, b_out)
    whole = lax.all_gather(own, "member", axis=0, tiled=True)
    assert UPDATES == 2
    for update in range(UPDATES):
        predicted = predict(inputs_pair, own, f_in, hid, outs, parity)
        collected = collect(predicted, n_samples, parity)
        mean_pred = jnp.mean(collected, axis=0)
        anomaly = (collected - mean_pred[None]).reshape(collected.shape[0], -1)
        misfit = (observed[None] + noise[update].astype(jnp.float32) - collected).reshape(
            collected.shape[0], -1
        )
        gram_part = lax.dot_general(
            anomaly, anomaly, (((1,), (1,)), ((), ())), precision=lax.Precision.HIGHEST
        )
        cross_part = lax.dot_general(
            anomaly, misfit, (((1,), (1,)), ((), ())), precision=lax.Precision.HIGHEST
        )
        h = gram_part.shape[0] // 2
        payload = jnp.concatenate(
            [gram_part[:h].reshape(-1), gram_part[h:, h:].reshape(-1), cross_part.reshape(-1)]
        )
        payload = gather_sum(gather_sum(payload, "dp"), "member")
        top = payload[: 2 * h * h].reshape(h, 2 * h)
        corner = payload[2 * h * h : 3 * h * h].reshape(h, h)
        gram = jnp.concatenate([top, jnp.concatenate([top[:, h:].T, corner], axis=1)], axis=0)
        sums = jnp.stack([gram, payload[3 * h * h :].reshape(cross_part.shape)])
        gain = solve_spd(sums, 1.0 / count, ridge_level, (whole,) if update == 0 else ())
        if update == 0:
            first_gain = gain
            columns = lax.dynamic_slice_in_dim(gain, first, per_device, 1)
            own = own + jnp.einsum("kj,kab->jab", columns, whole, precision=lax.Precision.HIGH)
        else:
            eye = jnp.eye(gain.shape[0], dtype=gain.dtype)
            through = jnp.dot(eye + first_gain, gain, precision=lax.Precision.HIGHEST)
            columns = lax.dynamic_slice_in_dim(through, first, per_device, 1)

            def part(rows, cut=None):
                base, src = own[:, rows], whole[:, rows]
                if cut is not None:
                    base, src = base[..., :cut], src[..., :cut]
                return base + jnp.einsum("kj,k...->j...", columns, src, precision=lax.Precision.HIGH)

            return (
                part(slice(0, f_in)),
                part(f_in + outs),
                part(slice(f_in, f_in + outs)),
                part(f_in + outs + 1, outs),
            )
    return unpack(own, f_in, hid, outs)


def solution(mesh):
    placed = (
        P("dp", None),
        P("member", "dp"),
        P(None, None, "member", "dp"),
        P("member", None, "dp"),
        P("member", "dp"),
        P("member", None, "dp"),
        P("member", None),
    )
    return jax.shard_map(
        on_device,
        mesh=mesh,
        in_specs=placed,
        out_specs=(
            P("member", None, "dp"),
            P("member", "dp"),
            P("member", None, "dp"),
            P("member", None),
        ),
        check_vma=False,
    )
```
